256 devices in a mesh: ctx: 4 (over y), exp: 64 (over z, x, core).
Axes of the slice: x: 4, y: 4, z: 8, core: 2. Of those that a mesh axis runs over, the one named last changes fastest.
Arguments:
- residual_in: bfloat16 [64, 256, 1536], P('exp', 'ctx'), may hold values from -6 to 6
- queries: bfloat16 [64, 256, 1536], P('exp', 'ctx'), may hold values from -6 to 6
- new_kv: bfloat16 [64, 256, 1024], P('exp', 'ctx'), may hold values from -6 to 6
- cache_kv: bfloat16 [64, 4096, 1024], P('exp', 'ctx'), may hold values from -6 to 6
- cache_len: int32 [64], P('exp'), may hold values from 1 to 4096, 133120 in all
- out_proj: bfloat16 [1536, 1536], replicated, may hold values from -0.625 to 0.625
- norm_gain: float32 [1536], replicated, may hold values from 0.1 to 1.9
- routes: int32 [64, 256, 6], P('exp', 'ctx'), may hold values from 0 to 63, all different within a row; in each aligned block of 64 rows (0 to 63, 64 to 127, ..., all dimensions but the last counted through in order) at most 9 rows name the same one
- route_w: bfloat16 [64, 256, 6], P('exp', 'ctx'), may hold values from 0.049804688 to 0.5
- w_gate_up: bfloat16 [64, 1536, 1024], P('exp'), may hold values from -0.15625 to 0.15625
- w_down: bfloat16 [64, 512, 1536], P('exp'), may hold values from -0.25 to 0.25
Outputs:
- layer_out: bfloat16 [64, 256, 1536], P('exp', 'ctx')
The draws below stay inside these ranges and needn't reach their ends.
Inputs may be any that keep to these rules, and one draw needn't show every extreme that they name: `cache_len`: the largest length is exactly 4096. `routes`: each token names 6 different experts; among the new tokens of one device (aligned blocks of 64 tokens) no expert is named by more than 9 tokens, a bound that some block reaches.
All inputs are finite; a program needn't handle non-finite values. No bound on the sum of `cache_len` on one device may be relied on, other than what follows from the above.
Results may differ from the reference program's by a relative error of at most 0.02.
Values may be sent and summed in bfloat16 or wider, within the bound.
No kernel may reach another device: no remote copies, remote signals or barrier semaphores. Data moves between devices by JAX's collectives and lax.ppermute only.
A program may use at most 128 MiB of HBM per device.

```python
import math
import jax
import jax.numpy as jnp
import numpy as np
from jax import lax

D = 1536
HEADS = 12
KVH = 4
HD = 128
FFE = 512
TOP = 6
Q_DEV = 64
EXPERTS = 64
GROUP = 3
REQS = 64
NEW = 256
CACHE = 4096
CAP = 9
N_CTX = 4


def draw_queries(key, part):
    shape = (REQS, NEW, HEADS * HD)
    base = jnp.clip(jax.random.normal(jax.random.fold_in(key, 11), shape, jnp.float32) * 1.5, -6.0, 6.0)
    return base.astype(jnp.bfloat16)


def draw_new_kv(key, part):
    shape = (REQS, NEW, 2 * KVH * HD)
    base = jnp.clip(jax.random.normal(jax.random.fold_in(key, 12), shape, jnp.float32), -6.0, 6.0)
    return base.astype(jnp.bfloat16)


def shard_levels(rng, shape, shards, smallest, largest):
    level, own = 1.0, jax.random.fold_in(rng, 6)
    for dim, shards_of in shards:
        steps = jnp.exp(jax.random.uniform(jax.random.fold_in(own, dim), (shards_of,), jnp.float32, smallest / len(shards), largest / len(shards)))
        level = level * jnp.repeat(steps, shape[dim] // shards_of).reshape([-1 if axis == dim else 1 for axis in range(len(shape))])
    return level


def profile(amount, total, reach, lean):
    portions = [(1 << 20) // math.isqrt(grade ** lean) + 1 for grade in range(2, amount + 1)]
    rest, given = total - reach - (amount - 1), [1] * (amount - 1)
    while rest > 0:
        movable = [i for i in range(amount - 1) if given[i] < reach]
        mass, budget = sum([portions[i] for i in movable]), rest
        for i in movable:
            more = min(reach - given[i], max(1, budget * portions[i] // mass), rest)
            given[i] = given[i] + more
            rest = rest - more
    return np.array([reach] + given)


def uneven_parts(stream_key, count, total, most, skew):
    if count == 2:
        one = jax.random.randint(stream_key, (), max(1, total - most), min(most, total - 1) + 1)
        return jnp.stack([one, total - one])
    tallies = jnp.asarray(profile(count, total, most, skew), jnp.int32)
    couples = (count - 1) // 2
    giver, sink = tallies[1:1 + 2 * couples:2], tallies[2:2 + 2 * couples:2]
    slack = jnp.minimum(giver - 1, most - sink)
    passed = jax.random.randint(jax.random.fold_in(stream_key, 1), (couples,), 0, 1 << 20) % (slack + 1)
    tallies = tallies.at[1:1 + 2 * couples:2].set(giver - passed).at[2:2 + 2 * couples:2].set(sink + passed)
    return tallies[jax.random.permutation(jax.random.fold_in(stream_key, 2), count)]


def assign_block(rng, own, number, rows, amount, top, reach, lean):
    order = jax.random.permutation(rng, amount)
    crowded, ordinary = load_shares(amount, rows * top, reach, lean, True), load_shares(amount, rows * top, reach, lean, False)
    places = jnp.arange(amount)

    def named(sizes, offset_by):
        used = int((sizes > 0).sum())
        fixed = max(1, used // 4)
        passed = fixed + (places - fixed + offset_by * (used - fixed)) % max(1, amount - fixed)
        return jnp.zeros((amount,), jnp.int32).at[order[jnp.where(places < fixed, places, passed)]].set(jnp.asarray(sizes, jnp.int32))

    sizes = jnp.where(number % 4 == 0, named(crowded, number // 4), named(ordinary, number - number // 4 - 1))
    mixed = jax.random.permutation(jax.random.fold_in(own, 3), amount)
    source_of, receiver = mixed[0:amount // 2 * 2:2], mixed[1:amount // 2 * 2:2]
    margin = jnp.minimum(sizes[source_of] - 1, reach - sizes[receiver]) // 2
    margin = jnp.where((source_of == order[0]) | (receiver == order[0]) | (sizes[receiver] == 0), 0, jnp.maximum(margin, 0))
    passed = jax.random.randint(jax.random.fold_in(own, 4), (amount // 2,), 0, 1 << 20) % (margin + 1)
    sizes = sizes.at[source_of].add(-passed).at[receiver].add(passed)
    labels = jnp.searchsorted(jnp.cumsum(sizes), jnp.arange(rows * top), side="right").astype(jnp.int32)
    listing = labels.reshape(top, rows).T
    listing = listing[jax.random.permutation(jax.random.fold_in(own, 1), rows)]
    offset_by = jax.random.randint(jax.random.fold_in(own, 2), (rows, 1), 0, top)
    return jnp.take_along_axis(listing, (jnp.arange(top)[None, :] + offset_by) % top, axis=1)


def load_shares(number_of, total, bound, skew, full):
    portions = [(1 << 20) // math.isqrt(grade ** skew) + 1 for grade in range(1, number_of + 1)]
    largest = bound if full else min(bound, max(-(-total // number_of), total * portions[0] // sum(portions)))
    least = 1 if total - largest >= number_of - 1 else 0
    given, rest = [largest] + [least] * (number_of - 1), total - largest - least * (number_of - 1)
    while rest > 0:
        free = [i for i in range(1, number_of) if given[i] < largest] or [i for i in range(1, number_of) if given[i] < bound]
        whole, remaining = sum([portions[i] for i in free]), rest
        for i in free:
            more = min(bound - given[i], max(1, remaining * portions[i] // whole), rest)
            given[i] = given[i] + more
            rest = rest - more
    return np.array(given)


def normal_values(stream_key, extent, deviation, reach, split=(), dtype=jnp.bfloat16):
    factor_of = shard_levels(stream_key, extent, split, -0.22, 0.18) if split else 1.0
    entries = jax.random.normal(stream_key, extent, jnp.float32) * deviation * factor_of
    return jnp.minimum(jnp.maximum(entries, -reach), reach).astype(dtype)


def setup_inputs(seed: int = 0) -> dict:
    key_list = jax.random.split(jax.random.key(seed), 12)
    residual_in = normal_values(key_list[0], (REQS, NEW, D), 1.0, 6.0, ((0, 64), (1, 4)))
    queries = draw_queries(jax.random.fold_in(key_list[11], 71), 0)
    new_kv = draw_new_kv(jax.random.fold_in(key_list[11], 71), 0)
    cache_kv = normal_values(key_list[3], (REQS, CACHE, 2 * KVH * HD), 1.0, 6.0, ((0, 64), (1, 4)))
    cache_len = uneven_parts(key_list[4], REQS, REQS * CACHE // 2 + CACHE // 2, CACHE, 2).astype(jnp.int32)
    out_proj = normal_values(key_list[5], (HEADS * HD, D), (D // 16) ** -0.5, 0.625)
    norm_gain = jnp.clip(1.0 + 0.18 * jax.random.normal(key_list[6], (D,), jnp.float32), 0.1, 1.9)
    routes_keys = jax.random.split(jax.random.fold_in(key_list[7], 1), REQS * NEW // Q_DEV)
    routes_turns = jax.random.permutation(jax.random.fold_in(key_list[7], 3), REQS * NEW // Q_DEV)
    routes = jax.vmap(lambda own, number: assign_block(jax.random.fold_in(key_list[7], 2), own, number, Q_DEV, EXPERTS, TOP, CAP, 1))(routes_keys, routes_turns).reshape((REQS, NEW, TOP))
    route_w = jnp.clip(0.049804688 + 0.4501953 * jax.random.uniform(key_list[8], (REQS, NEW, TOP), jnp.float32) ** shard_levels(key_list[8], (REQS, NEW, TOP), ((0, 64), (1, 4)), -0.2, 0.2), 0.049804688, 0.5).astype(jnp.bfloat16)
    w_gate_up = normal_values(key_list[9], (EXPERTS, D, 2 * FFE), D ** -0.5, 0.15625, ((0, 64),))
    w_down = normal_values(key_list[10], (EXPERTS, FFE, D), FFE ** -0.5, 0.25, ((0, 64),))
    return dict(residual_in=residual_in, queries=queries, new_kv=new_kv, cache_kv=cache_kv, cache_len=cache_len, out_proj=out_proj, norm_gain=norm_gain, routes=routes, route_w=route_w, w_gate_up=w_gate_up, w_down=w_down)


NEG_BIG = -1e+30

def attend_one(query_rows, new_rows, cache_rows, length):
    query_grid = query_rows.astype(jnp.float32).reshape(NEW, KVH, GROUP, HD)
    key_rows = jnp.concatenate([cache_rows, new_rows], 0).astype(jnp.float32)
    key_part = key_rows[:, :KVH * HD].reshape(-1, KVH, HD)
    value_part = key_rows[:, KVH * HD:].reshape(-1, KVH, HD)
    scores = jnp.einsum('qkgd,rkd->kgqr', query_grid, key_part) * HD ** (-0.5)
    cache_pos = jnp.arange(CACHE)
    new_pos = jnp.arange(NEW)
    usable = jnp.concatenate([jnp.broadcast_to((cache_pos < length)[None, :], (NEW, CACHE)), new_pos[None, :] <= new_pos[:, None]], 1)
    row_max = lax.optimization_barrier(jnp.max(jnp.where(usable, scores, NEG_BIG), -1))
    softmax_terms = jnp.where(usable, jnp.exp(scores - row_max[..., None]), 0.0)
    weight_sum = lax.optimization_barrier(jnp.sum(softmax_terms, -1))
    softmax_low = lax.optimization_barrier(softmax_terms.astype(jnp.bfloat16)).astype(jnp.float32)
    numerator = jnp.einsum('kgqr,rkd->kgqd', softmax_low, value_part)
    attended = numerator / weight_sum[..., None]
    return attended.transpose(2, 0, 1, 3).reshape(NEW, HEADS * HD).astype(jnp.bfloat16)

def reference(residual_in, queries, new_kv, cache_kv, cache_len, out_proj, norm_gain, routes, route_w, w_gate_up, w_down):
    attended = lax.map(lambda packed: attend_one(*packed), (queries, new_kv, cache_kv, cache_len))
    flat_in = residual_in.reshape(-1, D)
    mixed = (flat_in.astype(jnp.float32) + jnp.dot(attended.reshape(-1, HEADS * HD), out_proj, preferred_element_type=jnp.float32)).astype(jnp.bfloat16)
    widened = lax.optimization_barrier(mixed).astype(jnp.float32)
    normed = (widened * lax.rsqrt(lax.optimization_barrier(jnp.mean(widened * widened, -1, keepdims=True)) + 1e-06) * norm_gain).astype(jnp.bfloat16)
    expert_ids = routes.reshape(-1).astype(jnp.int32)
    token_ids = (jnp.arange(expert_ids.shape[0]) // TOP).astype(jnp.int32)
    gate_flat = route_w.reshape(-1).astype(jnp.float32)
    most_rows = REQS * N_CTX * CAP

    def one_expert(totals, expert):
        chosen = jnp.nonzero(expert_ids == expert, size=most_rows, fill_value=0)[0].astype(jnp.int32)
        live = jnp.arange(most_rows) < jnp.sum((expert_ids == expert).astype(jnp.int32))
        row_tokens = token_ids[chosen]
        gate_up = jnp.dot(normed[row_tokens], w_gate_up[expert], preferred_element_type=jnp.float32)
        activated = (jax.nn.silu(gate_up[:, :FFE]) * gate_up[:, FFE:]).astype(jnp.bfloat16)
        expert_out = jnp.dot(activated, w_down[expert], preferred_element_type=jnp.float32).astype(jnp.bfloat16)
        expert_wide = lax.optimization_barrier(expert_out).astype(jnp.float32)
        contrib = jnp.where(live[:, None], gate_flat[chosen][:, None] * expert_wide, 0.0)
        return (totals.at[row_tokens].add(contrib), None)
    totals, _ = lax.scan(one_expert, jnp.zeros((flat_in.shape[0], D), jnp.float32), jnp.arange(EXPERTS).astype(jnp.int32))
    layer_out = (widened + totals).astype(jnp.bfloat16)
    return layer_out.reshape(REQS, NEW, D)
```

```python
import jax
import jax.numpy as jnp
from jax import lax
from jax.sharding import PartitionSpec as P

D = 1536
KVH = 4
HD = 128
GROUP = 3


NEG_BIG = -1e30


def local(
    residual_in,
    queries,
    new_kv,
    cache_kv,
    cache_len,
    out_proj,
    norm_gain,
    routes,
    route_w,
    w_gate_up,
    w_down,
):
    tok_count = residual_in.shape[1]
    cache_rows = cache_kv.shape[1]
    n_ctx = lax.axis_size("ctx")
    ctx_pos = lax.axis_index("ctx")
    length = cache_len[0]
    score_scale = HD ** (-0.5)
    heads = KVH * GROUP

    all_queries = lax.all_gather(queries[0], "ctx", axis=0, tiled=True)
    query_total = all_queries.shape[0]
    query_grid = all_queries.reshape(query_total, KVH, GROUP, HD)
    local_keys = jnp.concatenate([cache_kv[0], new_kv[0]], 0)
    key_rows = local_keys.shape[0]
    key_width = local_keys.shape[1] // 2
    key_part = local_keys[:, :key_width].reshape(key_rows, KVH, HD)
    value_part = local_keys[:, key_width:].reshape(key_rows, KVH, HD)
    scores = (
        jnp.einsum("qkgd,rkd->kgqr", query_grid, key_part, preferred_element_type=jnp.float32)
        * score_scale
    )
    row_index = jnp.arange(key_rows)
    cached = row_index < cache_rows
    cache_pos = ctx_pos * cache_rows + row_index
    new_pos = ctx_pos * tok_count + row_index - cache_rows
    query_pos = jnp.arange(query_total)
    usable = jnp.where(
        cached[None, :], (cache_pos < length)[None, :], new_pos[None, :] <= query_pos[:, None]
    )
    part_max = jnp.max(jnp.where(usable, scores, NEG_BIG), -1)
    softmax_terms = jnp.where(usable, jnp.exp(scores - part_max[..., None]), 0.0)
    part_sum = jnp.sum(softmax_terms, -1)
    part_acc = jnp.einsum(
        "kgqr,rkd->qkgd",
        softmax_terms.astype(jnp.bfloat16),
        value_part,
        preferred_element_type=jnp.float32,
    )
    part_acc = part_acc.reshape(n_ctx, tok_count, heads, HD)
    stats = jnp.stack([part_max, part_sum], 0).reshape(2, heads, n_ctx, tok_count)
    stats = stats.transpose(2, 3, 1, 0).reshape(n_ctx, tok_count, heads * 2)
    got_acc = lax.all_to_all(part_acc, "ctx", split_axis=0, concat_axis=0, tiled=True)
    got_stats = lax.all_to_all(stats, "ctx", split_axis=0, concat_axis=0, tiled=True)
    got_stats = got_stats.reshape(n_ctx, tok_count, heads, 2)
    got_max = got_stats[..., 0]
    got_sum = got_stats[..., 1]
    top_max = jnp.max(got_max, 0)
    rescale = jnp.exp(got_max - top_max[None])
    total_sum = jnp.sum(rescale * got_sum, 0)
    total_acc = jnp.sum(rescale[..., None] * got_acc, 0)
    attended = (total_acc / total_sum[..., None]).reshape(tok_count, heads * HD)
    attended = attended.astype(jnp.bfloat16)
    mixed = (
        residual_in[0].astype(jnp.float32)
        + jnp.dot(attended, out_proj, preferred_element_type=jnp.float32)
    ).astype(jnp.bfloat16)
    widened = mixed.astype(jnp.float32)
    normed = (
        widened * lax.rsqrt(jnp.mean(widened * widened, -1, keepdims=True) + 1e-06) * norm_gain
    ).astype(jnp.bfloat16)
    top_count = routes.shape[2]
    local_experts = w_gate_up.shape[0]
    expert_total = local_experts * lax.axis_size("exp")
    capacity = min(tok_count, 3 * tok_count * top_count // (2 * expert_total))
    expert_ids = routes[0].reshape(-1)
    one_hot = (expert_ids[:, None] == jnp.arange(expert_total)[None, :]).astype(jnp.int32)
    before = jnp.cumsum(one_hot, 0) - one_hot
    slot_index = jnp.sum(before * one_hot, 1)
    dest = (expert_ids * capacity + slot_index).reshape(tok_count, top_count)
    slot_ids = jnp.arange(expert_total * capacity)
    hits = dest[None, :, :] == slot_ids[:, None, None]
    select = jnp.any(hits, -1).astype(jnp.bfloat16)
    outgoing = jnp.dot(select, normed, preferred_element_type=jnp.float32).astype(jnp.bfloat16)
    outgoing = outgoing.reshape(expert_total, capacity, D)
    hidden_half = w_gate_up.shape[2] // 2
    incoming = lax.all_to_all(outgoing, "exp", split_axis=0, concat_axis=0, tiled=True)
    item_count = incoming.shape[1]
    grouped = incoming.reshape(-1, local_experts, item_count, incoming.shape[2])
    gate_up = jnp.einsum("sekd,edf->sekf", grouped, w_gate_up, preferred_element_type=jnp.float32)
    activated = (jax.nn.silu(gate_up[..., :hidden_half]) * gate_up[..., hidden_half:]).astype(
        jnp.bfloat16
    )
    result = jnp.einsum(
        "sekf,efd->sekd", activated, w_down, preferred_element_type=jnp.float32
    ).astype(jnp.bfloat16)
    returned = lax.all_to_all(
        result.reshape(incoming.shape), "exp", split_axis=0, concat_axis=0, tiled=True
    )
    weights = route_w[0]
    combine = jnp.sum(
        jnp.where(hits.transpose(1, 0, 2), weights[:, None, :], jnp.zeros((), weights.dtype)), -1
    )
    blended = jnp.dot(
        combine, returned.reshape(-1, D), preferred_element_type=jnp.float32
    )
    return (widened + blended).astype(jnp.bfloat16)[None]


def solution(mesh):
    return jax.shard_map(
        local,
        mesh=mesh,
        in_specs=(
            P("exp", "ctx", None),
            P("exp", "ctx", None),
            P("exp", "ctx", None),
            P("exp", "ctx", None),
            P("exp"),
            P(),
            P(),
            P("exp", "ctx", None),
            P("exp", "ctx", None),
            P("exp", None, None),
            P("exp", None, None),
        ),
        out_specs=P("exp", "ctx", None),
        check_vma=False,
    )
```

```python
import jax
import jax.numpy as jnp
from jax import lax
from jax.sharding import Mesh, PartitionSpec as P

D = 1536
KVH = 4
HD = 128
GROUP = 3


NEG_BIG = -1e30


EXP_AXES = ("z", "x", "core")
CHIP_AXES = ("z", "x")


def dispatch(rows):
    split = rows.reshape(-1, 2, *rows.shape[1:])
    split = lax.all_to_all(split, "core", split_axis=1, concat_axis=1, tiled=True)
    split = lax.all_to_all(split, CHIP_AXES, split_axis=0, concat_axis=0, tiled=True)
    return split.reshape(rows.shape)


def undispatch(rows):
    split = rows.reshape(-1, 2, *rows.shape[1:])
    split = lax.all_to_all(split, CHIP_AXES, split_axis=0, concat_axis=0, tiled=True)
    split = lax.all_to_all(split, "core", split_axis=1, concat_axis=1, tiled=True)
    return split.reshape(rows.shape)


def local(
    residual_in,
    queries,
    new_kv,
    cache_kv,
    cache_len,
    out_proj,
    norm_gain,
    routes,
    route_w,
    w_gate_up,
    w_down,
):
    tok_count = residual_in.shape[1]
    cache_rows = cache_kv.shape[1]
    n_ctx = lax.axis_size("ctx")
    ctx_pos = lax.axis_index("ctx")
    length = cache_len[0]
    score_scale = HD ** (-0.5)
    heads = KVH * GROUP

    all_queries = lax.all_gather(queries[0], "ctx", axis=0, tiled=True)
    query_total = all_queries.shape[0]
    query_grid = all_queries.reshape(query_total, KVH, GROUP, HD)
    local_keys = jnp.concatenate([cache_kv[0], new_kv[0]], 0)
    key_rows = local_keys.shape[0]
    key_width = local_keys.shape[1] // 2
    key_part = local_keys[:, :key_width].reshape(key_rows, KVH, HD)
    value_part = local_keys[:, key_width:].reshape(key_rows, KVH, HD)
    scores = (
        jnp.einsum("qkgd,rkd->kgqr", query_grid, key_part, preferred_element_type=jnp.float32)
        * score_scale
    )
    row_index = jnp.arange(key_rows)
    cached = row_index < cache_rows
    cache_pos = ctx_pos * cache_rows + row_index
    new_pos = ctx_pos * tok_count + row_index - cache_rows
    query_pos = jnp.arange(query_total)
    usable = jnp.where(
        cached[None, :], (cache_pos < length)[None, :], new_pos[None, :] <= query_pos[:, None]
    )
    part_max = jnp.max(jnp.where(usable, scores, NEG_BIG), -1)
    softmax_terms = jnp.where(usable, jnp.exp(scores - part_max[..., None]), 0.0)
    part_sum = jnp.sum(softmax_terms, -1)
    part_acc = jnp.einsum(
        "kgqr,rkd->qkgd",
        softmax_terms.astype(jnp.bfloat16),
        value_part,
        preferred_element_type=jnp.float32,
    )
    part_acc = part_acc.reshape(n_ctx, tok_count, heads, HD)
    stats = jnp.stack([part_max, part_sum], 0).reshape(2, heads, n_ctx, tok_count)
    stats = stats.transpose(2, 3, 1, 0).reshape(n_ctx, tok_count, heads * 2)
    got_acc = lax.all_to_all(part_acc, "ctx", split_axis=0, concat_axis=0, tiled=True)
    got_stats = lax.all_to_all(stats, "ctx", split_axis=0, concat_axis=0, tiled=True)
    got_stats = got_stats.reshape(n_ctx, tok_count, heads, 2)
    got_max = got_stats[..., 0]
    got_sum = got_stats[..., 1]
    top_max = jnp.max(got_max, 0)
    rescale = jnp.exp(got_max - top_max[None])
    total_sum = jnp.sum(rescale * got_sum, 0)
    total_acc = jnp.sum(rescale[..., None] * got_acc, 0)
    attended = (total_acc / total_sum[..., None]).reshape(tok_count, heads * HD)
    attended = attended.astype(jnp.bfloat16)
    mixed = (
        residual_in[0].astype(jnp.float32)
        + jnp.dot(attended, out_proj, preferred_element_type=jnp.float32)
    ).astype(jnp.bfloat16)
    widened = mixed.astype(jnp.float32)
    normed = (
        widened * lax.rsqrt(jnp.mean(widened * widened, -1, keepdims=True) + 1e-06) * norm_gain
    ).astype(jnp.bfloat16)
    top_count = routes.shape[2]
    local_experts = w_gate_up.shape[0]
    expert_total = local_experts * lax.axis_size(EXP_AXES)
    capacity = min(tok_count, 3 * tok_count * top_count // (2 * expert_total))
    expert_ids = routes[0].reshape(-1)
    one_hot = (expert_ids[:, None] == jnp.arange(expert_total)[None, :]).astype(jnp.int32)
    before = jnp.cumsum(one_hot, 0) - one_hot
    slot_index = jnp.sum(before * one_hot, 1)
    dest = (expert_ids * capacity + slot_index).reshape(tok_count, top_count)
    slot_ids = jnp.arange(expert_total * capacity)
    hits = dest[None, :, :] == slot_ids[:, None, None]
    select = jnp.any(hits, -1).astype(jnp.bfloat16)
    outgoing = jnp.dot(select, normed, preferred_element_type=jnp.float32).astype(jnp.bfloat16)
    outgoing = outgoing.reshape(expert_total, capacity, D)
    hidden_half = w_gate_up.shape[2] // 2
    incoming = dispatch(outgoing)
    item_count = incoming.shape[1]
    grouped = incoming.reshape(-1, local_experts, item_count, incoming.shape[2])
    gate_up = jnp.einsum("sekd,edf->sekf", grouped, w_gate_up, preferred_element_type=jnp.float32)
    activated = (jax.nn.silu(gate_up[..., :hidden_half]) * gate_up[..., hidden_half:]).astype(
        jnp.bfloat16
    )
    result = jnp.einsum(
        "sekf,efd->sekd", activated, w_down, preferred_element_type=jnp.float32
    ).astype(jnp.bfloat16)
    returned = undispatch(result.reshape(incoming.shape))
    weights = route_w[0]
    combine = jnp.sum(
        jnp.where(hits.transpose(1, 0, 2), weights[:, None, :], jnp.zeros((), weights.dtype)), -1
    )
    blended = jnp.dot(
        combine, returned.reshape(-1, D), preferred_element_type=jnp.float32
    )
    return (widened + blended).astype(jnp.bfloat16)[None]


def solution(mesh):
    exp_size = mesh.shape["exp"]
    x_size, core_size = 4, 2
    devices = mesh.devices.reshape(
        mesh.shape["ctx"], exp_size // (x_size * core_size), x_size, core_size
    )
    fine = Mesh(devices, ("ctx",) + EXP_AXES)
    rows = P(EXP_AXES, "ctx", None)
    return jax.shard_map(
        local,
        mesh=fine,
        in_specs=(
            rows,
            rows,
            rows,
            rows,
            P(EXP_AXES),
            P(),
            P(),
            rows,
            rows,
            P(EXP_AXES, None, None),
            P(EXP_AXES, None, None),
        ),
        out_specs=rows,
        check_vma=False,
    )
```

```python
import jax
import jax.numpy as jnp
from jax import lax
from jax.experimental import pallas as pl
from jax.experimental.pallas import tpu as pltpu
from jax.sharding import Mesh, PartitionSpec as P

D = 1536
KVH = 4
HD = 128
GROUP = 3


NEG_BIG = -1e30


def attend_kernel(scal_ref, q_ref, kc_ref, vc_ref, kn_ref, vn_ref, acc_ref, st_ref):
    ctx_pos = scal_ref[0]
    length = scal_ref[1]
    scale = HD ** (-0.5)
    q = q_ref[...]
    dims = (((1,), (1,)), ((), ()))
    s_c = lax.dot_general(q, kc_ref[...], dims, preferred_element_type=jnp.float32) * scale
    s_n = lax.dot_general(q, kn_ref[...], dims, preferred_element_type=jnp.float32) * scale
    n_q, n_cache = s_c.shape
    n_new = s_n.shape[1]
    use_c = ctx_pos * n_cache + lax.broadcasted_iota(jnp.int32, (n_q, n_cache), 1) < length
    use_n = ctx_pos * n_new + lax.broadcasted_iota(jnp.int32, (n_q, n_new), 1) <= (
        lax.broadcasted_iota(jnp.int32, (n_q, n_new), 0)
    )
    top = jnp.maximum(
        jnp.max(jnp.where(use_c, s_c, NEG_BIG), 1, keepdims=True),
        jnp.max(jnp.where(use_n, s_n, NEG_BIG), 1, keepdims=True),
    )
    p_c = jnp.where(use_c, jnp.exp(s_c - top), 0.0)
    p_n = jnp.where(use_n, jnp.exp(s_n - top), 0.0)
    total = jnp.sum(p_c, 1, keepdims=True) + jnp.sum(p_n, 1, keepdims=True)
    acc_ref[...] = jnp.dot(
        p_c.astype(jnp.bfloat16), vc_ref[...], preferred_element_type=jnp.float32
    ) + jnp.dot(p_n.astype(jnp.bfloat16), vn_ref[...], preferred_element_type=jnp.float32)
    lane = lax.broadcasted_iota(jnp.int32, acc_ref.shape, 1)
    st_ref[...] = jnp.where(lane < 64, top, total)


def partial_attention(scal, all_queries, cache_rows, new_rows):
    n_q = all_queries.shape[0]
    n_cache = cache_rows.shape[0]
    n_new = new_rows.shape[0]
    heads = KVH * GROUP
    q_spec = pl.BlockSpec((n_q, HD), lambda k, g, s: (0, k * GROUP + g))
    out_shape = jax.ShapeDtypeStruct((n_q, heads * HD), jnp.float32)
    cost = pl.CostEstimate(
        flops=4 * n_q * (n_cache + n_new) * HD * heads,
        transcendentals=n_q * (n_cache + n_new) * heads,
        bytes_accessed=2 * (all_queries.size + cache_rows.size + new_rows.size) + 8 * n_q * heads * HD,
    )
    return pl.pallas_call(
        attend_kernel,
        out_shape=(out_shape, out_shape),
        grid_spec=pltpu.PrefetchScalarGridSpec(
            num_scalar_prefetch=1,
            grid=(KVH, GROUP),
            in_specs=[
                q_spec,
                pl.BlockSpec((n_cache, HD), lambda k, g, s: (0, k)),
                pl.BlockSpec((n_cache, HD), lambda k, g, s: (0, KVH + k)),
                pl.BlockSpec((n_new, HD), lambda k, g, s: (0, k)),
                pl.BlockSpec((n_new, HD), lambda k, g, s: (0, KVH + k)),
            ],
            out_specs=[q_spec, q_spec],
        ),
        cost_estimate=cost,
    )(scal, all_queries, cache_rows, cache_rows, new_rows, new_rows)


EXP_AXES = ("z", "x", "core")
CHIP_AXES = ("z", "x")


def dispatch(rows):
    split = rows.reshape(-1, 2, *rows.shape[1:])
    split = lax.all_to_all(split, "core", split_axis=1, concat_axis=1, tiled=True)
    split = lax.all_to_all(split, CHIP_AXES, split_axis=0, concat_axis=0, tiled=True)
    return split.reshape(rows.shape)


def undispatch(rows):
    split = rows.reshape(-1, 2, *rows.shape[1:])
    split = lax.all_to_all(split, CHIP_AXES, split_axis=0, concat_axis=0, tiled=True)
    split = lax.all_to_all(split, "core", split_axis=1, concat_axis=1, tiled=True)
    return split.reshape(rows.shape)


def local(
    residual_in,
    queries,
    new_kv,
    cache_kv,
    cache_len,
    out_proj,
    norm_gain,
    routes,
    route_w,
    w_gate_up,
    w_down,
):
    tok_count = residual_in.shape[1]
    cache_rows = cache_kv.shape[1]
    n_ctx = lax.axis_size("ctx")
    ctx_pos = lax.axis_index("ctx")
    length = cache_len[0]
    score_scale = HD ** (-0.5)
    heads = KVH * GROUP

    all_queries = lax.all_gather(queries[0], "ctx", axis=0, tiled=True)
    scal = jnp.stack([ctx_pos, length]).astype(jnp.int32)
    part_acc, part_stats = partial_attention(scal, all_queries, cache_kv[0], new_kv[0])
    part_stats = part_stats.reshape(n_ctx * tok_count, heads, HD)
    stats = jnp.concatenate([part_stats[:, :, 0], part_stats[:, :, 64]], -1)
    got_acc = lax.all_to_all(
        part_acc.reshape(n_ctx, tok_count, heads * HD), "ctx", split_axis=0, concat_axis=0, tiled=True
    )
    got_stats = lax.all_to_all(
        stats.reshape(n_ctx, tok_count, 2 * heads), "ctx", split_axis=0, concat_axis=0, tiled=True
    )
    got_max = got_stats[..., :heads]
    got_sum = got_stats[..., heads:]
    top_max = jnp.max(got_max, 0)
    rescale = jnp.exp(got_max - top_max[None])
    total_sum = jnp.sum(rescale * got_sum, 0)
    total_acc = jnp.sum(rescale[..., None] * got_acc.reshape(n_ctx, tok_count, heads, HD), 0)
    attended = (total_acc / total_sum[..., None]).reshape(tok_count, heads * HD)
    attended = attended.astype(jnp.bfloat16)
    mixed = (
        residual_in[0].astype(jnp.float32)
        + jnp.dot(attended, out_proj, preferred_element_type=jnp.float32)
    ).astype(jnp.bfloat16)
    widened = mixed.astype(jnp.float32)
    normed = (
        widened * lax.rsqrt(jnp.mean(widened * widened, -1, keepdims=True) + 1e-06) * norm_gain
    ).astype(jnp.bfloat16)
    top_count = routes.shape[2]
    local_experts = w_gate_up.shape[0]
    expert_total = local_experts * lax.axis_size(EXP_AXES)
    capacity = min(tok_count, 3 * tok_count * top_count // (2 * expert_total))
    expert_ids = routes[0].reshape(-1)
    one_hot = (expert_ids[:, None] == jnp.arange(expert_total)[None, :]).astype(jnp.int32)
    before = jnp.cumsum(one_hot, 0) - one_hot
    slot_index = jnp.sum(before * one_hot, 1)
    dest = (expert_ids * capacity + slot_index).reshape(tok_count, top_count)
    slot_ids = jnp.arange(expert_total * capacity)
    hits = dest[None, :, :] == slot_ids[:, None, None]
    select = jnp.any(hits, -1).astype(jnp.bfloat16)
    outgoing = jnp.dot(select, normed, preferred_element_type=jnp.float32).astype(jnp.bfloat16)
    outgoing = outgoing.reshape(expert_total, capacity, D)
    hidden_half = w_gate_up.shape[2] // 2
    incoming = dispatch(outgoing)
    item_count = incoming.shape[1]
    grouped = incoming.reshape(-1, local_experts, item_count, incoming.shape[2])
    gate_up = jnp.einsum("sekd,edf->sekf", grouped, w_gate_up, preferred_element_type=jnp.float32)
    activated = (jax.nn.silu(gate_up[..., :hidden_half]) * gate_up[..., hidden_half:]).astype(
        jnp.bfloat16
    )
    result = jnp.einsum(
        "sekf,efd->sekd", activated, w_down, preferred_element_type=jnp.float32
    ).astype(jnp.bfloat16)
    returned = undispatch(result.reshape(incoming.shape))
    weights = route_w[0]
    combine = jnp.sum(
        jnp.where(hits.transpose(1, 0, 2), weights[:, None, :], jnp.zeros((), weights.dtype)), -1
    )
    blended = jnp.dot(
        combine, returned.reshape(-1, D), preferred_element_type=jnp.float32
    )
    return (widened + blended).astype(jnp.bfloat16)[None]


def solution(mesh):
    exp_size = mesh.shape["exp"]
    x_size, core_size = 4, 2
    devices = mesh.devices.reshape(
        mesh.shape["ctx"], exp_size // (x_size * core_size), x_size, core_size
    )
    fine = Mesh(devices, ("ctx",) + EXP_AXES)
    rows = P(EXP_AXES, "ctx", None)
    return jax.shard_map(
        local,
        mesh=fine,
        in_specs=(
            rows,
            rows,
            rows,
            rows,
            P(EXP_AXES),
            P(),
            P(),
            rows,
            rows,
            P(EXP_AXES, None, None),
            P(EXP_AXES, None, None),
        ),
        out_specs=rows,
        check_vma=False,
    )
```

```python
import jax
import jax.numpy as jnp
from jax import lax
from jax.experimental import pallas as pl
from jax.experimental.pallas import tpu as pltpu
from jax.sharding import Mesh, PartitionSpec as P

D = 1536
KVH = 4
HD = 128
GROUP = 3


NEG_BIG = -1e30


def attend_kernel(scal_ref, q_ref, kc_ref, vc_ref, kn_ref, vn_ref, out_ref):
    head = pl.program_id(0) * GROUP + pl.program_id(1)
    heads = KVH * GROUP
    ctx_pos = scal_ref[0]
    length = scal_ref[1]
    scale = HD ** (-0.5)
    q = q_ref[...]
    dims = (((1,), (1,)), ((), ()))
    s_c = lax.dot_general(q, kc_ref[...], dims, preferred_element_type=jnp.float32) * scale
    s_n = lax.dot_general(q, kn_ref[...], dims, preferred_element_type=jnp.float32) * scale
    n_q, n_cache = s_c.shape
    n_new = s_n.shape[1]
    use_c = ctx_pos * n_cache + lax.broadcasted_iota(jnp.int32, (n_q, n_cache), 1) < length
    use_n = ctx_pos * n_new + lax.broadcasted_iota(jnp.int32, (n_q, n_new), 1) <= (
        lax.broadcasted_iota(jnp.int32, (n_q, n_new), 0)
    )
    top = jnp.maximum(
        jnp.max(jnp.where(use_c, s_c, NEG_BIG), 1, keepdims=True),
        jnp.max(jnp.where(use_n, s_n, NEG_BIG), 1, keepdims=True),
    )
    p_c = jnp.where(use_c, jnp.exp(s_c - top), 0.0)
    p_n = jnp.where(use_n, jnp.exp(s_n - top), 0.0)
    total = jnp.sum(p_c, 1, keepdims=True) + jnp.sum(p_n, 1, keepdims=True)
    acc = jnp.dot(
        p_c.astype(jnp.bfloat16), vc_ref[...], preferred_element_type=jnp.float32
    ) + jnp.dot(p_n.astype(jnp.bfloat16), vn_ref[...], preferred_element_type=jnp.float32)
    out_ref[:, pl.ds(pl.multiple_of(head * HD, HD), HD)] = acc
    stat_cols = slice(heads * HD, (heads + 1) * HD)

    @pl.when(head == 0)
    def _():
        out_ref[:, stat_cols] = jnp.zeros((n_q, HD), jnp.float32)

    lane = lax.broadcasted_iota(jnp.int32, (n_q, HD), 1)
    held = out_ref[:, stat_cols]
    out_ref[:, stat_cols] = jnp.where(lane == head, top, jnp.where(lane == heads + head, total, held))


def partial_attention(scal, all_queries, cache_rows, new_rows):
    n_q = all_queries.shape[0]
    n_cache = cache_rows.shape[0]
    n_new = new_rows.shape[0]
    heads = KVH * GROUP
    width = (heads + 1) * HD
    cost = pl.CostEstimate(
        flops=4 * n_q * (n_cache + n_new) * HD * heads,
        transcendentals=n_q * (n_cache + n_new) * heads,
        bytes_accessed=2 * (all_queries.size + cache_rows.size + new_rows.size) + 4 * n_q * width,
    )
    return pl.pallas_call(
        attend_kernel,
        out_shape=jax.ShapeDtypeStruct((n_q, width), jnp.float32),
        grid_spec=pltpu.PrefetchScalarGridSpec(
            num_scalar_prefetch=1,
            grid=(KVH, GROUP),
            in_specs=[
                pl.BlockSpec((n_q, HD), lambda k, g, s: (0, k * GROUP + g)),
                pl.BlockSpec((n_cache, HD), lambda k, g, s: (0, k)),
                pl.BlockSpec((n_cache, HD), lambda k, g, s: (0, KVH + k)),
                pl.BlockSpec((n_new, HD), lambda k, g, s: (0, k)),
                pl.BlockSpec((n_new, HD), lambda k, g, s: (0, KVH + k)),
            ],
            out_specs=pl.BlockSpec((n_q, width), lambda k, g, s: (0, 0)),
        ),
        cost_estimate=cost,
    )(scal, all_queries, cache_rows, cache_rows, new_rows, new_rows)


EXP_AXES = ("z", "x", "core")
CHIP_AXES = ("z", "x")


def local(
    residual_in,
    queries,
    new_kv,
    cache_kv,
    cache_len,
    out_proj,
    norm_gain,
    routes,
    route_w,
    w_gate_up,
    w_down,
):
    tok_count = residual_in.shape[1]
    cache_rows = cache_kv.shape[1]
    n_ctx = lax.axis_size("ctx")
    ctx_pos = lax.axis_index("ctx")
    length = cache_len[0]
    score_scale = HD ** (-0.5)
    heads = KVH * GROUP

    all_queries = lax.all_gather(queries[0], "ctx", axis=0, tiled=True)
    scal = jnp.stack([ctx_pos, length]).astype(jnp.int32)
    part = partial_attention(scal, all_queries, cache_kv[0], new_kv[0])
    got = lax.all_to_all(
        part.reshape(n_ctx, tok_count, part.shape[1]), "ctx", split_axis=0, concat_axis=0, tiled=True
    )
    got_acc = got[..., : heads * HD].reshape(n_ctx, tok_count, heads, HD)
    got_max = got[..., heads * HD : heads * HD + heads]
    got_sum = got[..., heads * HD + heads : heads * HD + 2 * heads]
    top_max = jnp.max(got_max, 0)
    rescale = jnp.exp(got_max - top_max[None])
    total_sum = jnp.sum(rescale * got_sum, 0)
    total_acc = jnp.sum(rescale[..., None] * got_acc, 0)
    attended = (total_acc / total_sum[..., None]).reshape(tok_count, heads * HD)
    attended = attended.astype(jnp.bfloat16)
    mixed = (
        residual_in[0].astype(jnp.float32)
        + jnp.dot(attended, out_proj, preferred_element_type=jnp.float32)
    ).astype(jnp.bfloat16)
    widened = mixed.astype(jnp.float32)
    normed = (
        widened * lax.rsqrt(jnp.mean(widened * widened, -1, keepdims=True) + 1e-06) * norm_gain
    ).astype(jnp.bfloat16)

    top_count = routes.shape[2]
    core_size = lax.axis_size("core")
    core_pos = lax.axis_index("core")
    expert_total = w_gate_up.shape[0] * lax.axis_size(EXP_AXES)
    capacity = min(tok_count, 3 * tok_count * top_count // (2 * expert_total))
    packed = jnp.concatenate(
        [
            normed,
            routes[0].astype(jnp.bfloat16),
            route_w[0],
            jnp.zeros((tok_count, HD - 2 * top_count), jnp.bfloat16),
        ],
        -1,
    )
    both = lax.all_gather(packed, "core", axis=0, tiled=True)
    normed_both = both[:, :D]
    routes_both = both[:, D : D + top_count].astype(jnp.int32)
    weights_both = both[:, D + top_count : D + 2 * top_count]
    expert_ids = routes_both.reshape(core_size, tok_count * top_count)
    one_hot = (expert_ids[..., None] == jnp.arange(expert_total)).astype(jnp.int32)
    before = jnp.cumsum(one_hot, 1) - one_hot
    slot_index = jnp.sum(before * one_hot, -1)
    block_rows = core_size * capacity
    source_core = jnp.arange(core_size)[:, None]
    dest = jnp.where(
        expert_ids % core_size == core_pos,
        (expert_ids // core_size) * block_rows + source_core * capacity + slot_index,
        -1,
    ).reshape(core_size * tok_count, top_count)
    chip_count = expert_total // core_size
    slot_ids = jnp.arange(chip_count * block_rows)
    hits = dest[None, :, :] == slot_ids[:, None, None]
    select = jnp.any(hits, -1).astype(jnp.bfloat16)
    outgoing = jnp.dot(select, normed_both, preferred_element_type=jnp.float32).astype(jnp.bfloat16)
    incoming = lax.all_to_all(
        outgoing.reshape(chip_count, block_rows, D), CHIP_AXES, split_axis=0, concat_axis=0, tiled=True
    ).reshape(-1, D)
    hidden_half = w_gate_up.shape[2] // 2
    gate_up = jnp.dot(incoming, w_gate_up[0], preferred_element_type=jnp.float32)
    activated = (jax.nn.silu(gate_up[:, :hidden_half]) * gate_up[:, hidden_half:]).astype(
        jnp.bfloat16
    )
    result = jnp.dot(activated, w_down[0], preferred_element_type=jnp.float32).astype(jnp.bfloat16)
    returned = lax.all_to_all(
        result.reshape(chip_count, block_rows, D), CHIP_AXES, split_axis=0, concat_axis=0, tiled=True
    ).reshape(-1, D)
    combine = jnp.sum(
        jnp.where(
            hits.transpose(1, 0, 2), weights_both[:, None, :], jnp.zeros((), weights_both.dtype)
        ),
        -1,
    )
    partial = jnp.dot(combine, returned, preferred_element_type=jnp.float32)
    blended = lax.psum_scatter(partial, "core", scatter_dimension=0, tiled=True)
    return (widened + blended).astype(jnp.bfloat16)[None]


def solution(mesh):
    exp_size = mesh.shape["exp"]
    x_size, core_size = 4, 2
    devices = mesh.devices.reshape(
        mesh.shape["ctx"], exp_size // (x_size * core_size), x_size, core_size
    )
    fine = Mesh(devices, ("ctx",) + EXP_AXES)
    rows = P(EXP_AXES, "ctx", None)
    return jax.shard_map(
        local,
        mesh=fine,
        in_specs=(
            rows,
            rows,
            rows,
            rows,
            P(EXP_AXES),
            P(),
            P(),
            rows,
            rows,
            P(EXP_AXES, None, None),
            P(EXP_AXES, None, None),
        ),
        out_specs=rows,
        check_vma=False,
    )
```

```python
import jax
import jax.numpy as jnp
from jax import lax
from jax.experimental import pallas as pl
from jax.experimental.pallas import tpu as pltpu
from jax.sharding import Mesh, PartitionSpec as P

D = 1536
KVH = 4
HD = 128
GROUP = 3


NEG_BIG = -1e30


def attend_kernel(scal_ref, q_ref, kc_ref, vc_ref, kn_ref, vn_ref, out_ref):
    head = pl.program_id(0) * GROUP + pl.program_id(1)
    heads = KVH * GROUP
    ctx_pos = scal_ref[0]
    length = scal_ref[1]
    scale = HD ** (-0.5)
    q = q_ref[...]
    dims = (((1,), (1,)), ((), ()))
    s_c = lax.dot_general(q, kc_ref[...], dims, preferred_element_type=jnp.float32) * scale
    s_n = lax.dot_general(q, kn_ref[...], dims, preferred_element_type=jnp.float32) * scale
    n_q, n_cache = s_c.shape
    n_new = s_n.shape[1]
    use_c = ctx_pos * n_cache + lax.broadcasted_iota(jnp.int32, (n_q, n_cache), 1) < length
    use_n = ctx_pos * n_new + lax.broadcasted_iota(jnp.int32, (n_q, n_new), 1) <= (
        lax.broadcasted_iota(jnp.int32, (n_q, n_new), 0)
    )
    top = jnp.maximum(
        jnp.max(jnp.where(use_c, s_c, NEG_BIG), 1, keepdims=True),
        jnp.max(jnp.where(use_n, s_n, NEG_BIG), 1, keepdims=True),
    )
    p_c = jnp.where(use_c, jnp.exp(s_c - top), 0.0)
    p_n = jnp.where(use_n, jnp.exp(s_n - top), 0.0)
    total = jnp.sum(p_c, 1, keepdims=True) + jnp.sum(p_n, 1, keepdims=True)
    acc = jnp.dot(
        p_c.astype(jnp.bfloat16), vc_ref[...], preferred_element_type=jnp.float32
    ) + jnp.dot(p_n.astype(jnp.bfloat16), vn_ref[...], preferred_element_type=jnp.float32)
    out_ref[:, pl.ds(pl.multiple_of(head * HD, HD), HD)] = acc.astype(out_ref.dtype)
    stat_cols = slice(heads * HD, (heads + 1) * HD)

    @pl.when(head == 0)
    def _():
        out_ref[:, stat_cols] = jnp.zeros((n_q, HD), out_ref.dtype)

    top_hi = top.astype(jnp.bfloat16).astype(jnp.float32)
    total_hi = total.astype(jnp.bfloat16).astype(jnp.float32)
    lane = lax.broadcasted_iota(jnp.int32, (n_q, HD), 1)
    held = out_ref[:, stat_cols].astype(jnp.float32)
    held = jnp.where(lane == head, top_hi, held)
    held = jnp.where(lane == heads + head, top - top_hi, held)
    held = jnp.where(lane == 2 * heads + head, total_hi, held)
    held = jnp.where(lane == 3 * heads + head, total - total_hi, held)
    out_ref[:, stat_cols] = held.astype(out_ref.dtype)


def partial_attention(scal, all_queries, cache_rows, new_rows):
    n_q = all_queries.shape[0]
    n_cache = cache_rows.shape[0]
    n_new = new_rows.shape[0]
    heads = KVH * GROUP
    width = (heads + 1) * HD
    cost = pl.CostEstimate(
        flops=4 * n_q * (n_cache + n_new) * HD * heads,
        transcendentals=n_q * (n_cache + n_new) * heads,
        bytes_accessed=2 * (all_queries.size + cache_rows.size + new_rows.size) + 2 * n_q * width,
    )
    return pl.pallas_call(
        attend_kernel,
        out_shape=jax.ShapeDtypeStruct((n_q, width), jnp.bfloat16),
        grid_spec=pltpu.PrefetchScalarGridSpec(
            num_scalar_prefetch=1,
            grid=(KVH, GROUP),
            in_specs=[
                pl.BlockSpec((n_q, HD), lambda k, g, s: (0, k * GROUP + g)),
                pl.BlockSpec((n_cache, HD), lambda k, g, s: (0, k)),
                pl.BlockSpec((n_cache, HD), lambda k, g, s: (0, KVH + k)),
                pl.BlockSpec((n_new, HD), lambda k, g, s: (0, k)),
                pl.BlockSpec((n_new, HD), lambda k, g, s: (0, KVH + k)),
            ],
            out_specs=pl.BlockSpec((n_q, width), lambda k, g, s: (0, 0)),
        ),
        cost_estimate=cost,
    )(scal, all_queries, cache_rows, cache_rows, new_rows, new_rows)


EXP_AXES = ("z", "x", "core")
CHIP_AXES = ("z", "x")


def local(
    residual_in,
    queries,
    new_kv,
    cache_kv,
    cache_len,
    out_proj,
    norm_gain,
    routes,
    route_w,
    w_gate_up,
    w_down,
):
    tok_count = residual_in.shape[1]
    cache_rows = cache_kv.shape[1]
    n_ctx = lax.axis_size("ctx")
    ctx_pos = lax.axis_index("ctx")
    length = cache_len[0]
    score_scale = HD ** (-0.5)
    heads = KVH * GROUP

    all_queries = lax.all_gather(queries[0], "ctx", axis=0, tiled=True)
    scal = jnp.stack([ctx_pos, length]).astype(jnp.int32)
    part = partial_attention(scal, all_queries, cache_kv[0], new_kv[0])
    got = lax.all_to_all(
        part.reshape(n_ctx, tok_count, part.shape[1]), "ctx", split_axis=0, concat_axis=0, tiled=True
    )
    got_acc = got[..., : heads * HD].astype(jnp.float32).reshape(n_ctx, tok_count, heads, HD)
    got_stats = got[..., heads * HD : heads * HD + 4 * heads].astype(jnp.float32)
    got_stats = got_stats.reshape(n_ctx, tok_count, 4, heads)
    got_max = got_stats[:, :, 0] + got_stats[:, :, 1]
    got_sum = got_stats[:, :, 2] + got_stats[:, :, 3]
    top_max = jnp.max(got_max, 0)
    rescale = jnp.exp(got_max - top_max[None])
    total_sum = jnp.sum(rescale * got_sum, 0)
    total_acc = jnp.sum(rescale[..., None] * got_acc, 0)
    attended = (total_acc / total_sum[..., None]).reshape(tok_count, heads * HD)
    attended = attended.astype(jnp.bfloat16)
    mixed = (
        residual_in[0].astype(jnp.float32)
        + jnp.dot(attended, out_proj, preferred_element_type=jnp.float32)
    ).astype(jnp.bfloat16)
    widened = mixed.astype(jnp.float32)
    normed = (
        widened * lax.rsqrt(jnp.mean(widened * widened, -1, keepdims=True) + 1e-06) * norm_gain
    ).astype(jnp.bfloat16)

    top_count = routes.shape[2]
    core_size = lax.axis_size("core")
    core_pos = lax.axis_index("core")
    expert_total = w_gate_up.shape[0] * lax.axis_size(EXP_AXES)
    capacity = min(tok_count, 3 * tok_count * top_count // (2 * expert_total))
    packed = jnp.concatenate(
        [
            normed,
            routes[0].astype(jnp.bfloat16),
            route_w[0],
            jnp.zeros((tok_count, HD - 2 * top_count), jnp.bfloat16),
        ],
        -1,
    )
    both = lax.all_gather(packed, "core", axis=0, tiled=True)
    normed_both = both[:, :D]
    routes_both = both[:, D : D + top_count].astype(jnp.int32)
    weights_both = both[:, D + top_count : D + 2 * top_count]
    expert_ids = routes_both.reshape(core_size, tok_count * top_count)
    one_hot = (expert_ids[..., None] == jnp.arange(expert_total)).astype(jnp.int32)
    before = jnp.cumsum(one_hot, 1) - one_hot
    slot_index = jnp.sum(before * one_hot, -1)
    block_rows = core_size * capacity
    source_core = jnp.arange(core_size)[:, None]
    dest = jnp.where(
        expert_ids % core_size == core_pos,
        ((expert_ids // core_size) * capacity + slot_index) * core_size + source_core,
        -1,
    ).reshape(core_size * tok_count, top_count)
    chip_count = expert_total // core_size
    slot_ids = jnp.arange(chip_count * block_rows)
    hits = dest[None, :, :] == slot_ids[:, None, None]
    slot_shape = (chip_count, capacity, core_size)
    select = jnp.any(hits, -1).astype(jnp.bfloat16).reshape(*slot_shape, -1)
    outgoing = jnp.einsum(
        "jscr,rd->jscd", select, normed_both, preferred_element_type=jnp.float32
    ).astype(jnp.bfloat16)
    incoming = lax.all_to_all(outgoing, CHIP_AXES, split_axis=0, concat_axis=0, tiled=True)
    hidden_half = w_gate_up.shape[2] // 2
    gate_up = jnp.einsum("jscd,df->jscf", incoming, w_gate_up[0], preferred_element_type=jnp.float32)
    activated = (jax.nn.silu(gate_up[..., :hidden_half]) * gate_up[..., hidden_half:]).astype(
        jnp.bfloat16
    )
    result = jnp.einsum(
        "jscf,fd->jscd", activated, w_down[0], preferred_element_type=jnp.float32
    ).astype(jnp.bfloat16)
    returned = lax.all_to_all(result, CHIP_AXES, split_axis=0, concat_axis=0, tiled=True)
    combine = jnp.sum(
        jnp.where(
            hits.transpose(1, 0, 2), weights_both[:, None, :], jnp.zeros((), weights_both.dtype)
        ),
        -1,
    ).reshape(-1, *slot_shape)
    partial = jnp.einsum("tjsc,jscd->td", combine, returned, preferred_element_type=jnp.float32)
    blended = lax.psum_scatter(partial, "core", scatter_dimension=0, tiled=True)
    return (widened + blended).astype(jnp.bfloat16)[None]


def solution(mesh):
    exp_size = mesh.shape["exp"]
    x_size, core_size = 4, 2
    devices = mesh.devices.reshape(
        mesh.shape["ctx"], exp_size // (x_size * core_size), x_size, core_size
    )
    fine = Mesh(devices, ("ctx",) + EXP_AXES)
    rows = P(EXP_AXES, "ctx", None)
    return jax.shard_map(
        local,
        mesh=fine,
        in_specs=(
            rows,
            rows,
            rows,
            rows,
            P(EXP_AXES),
            P(),
            P(),
            rows,
            rows,
            P(EXP_AXES, None, None),
            P(EXP_AXES, None, None),
        ),
        out_specs=rows,
        check_vma=False,
    )
```

```python
import jax
import jax.numpy as jnp
from jax import lax
from jax.experimental import pallas as pl
from jax.experimental.pallas import tpu as pltpu
from jax.sharding import Mesh, PartitionSpec as P

D = 1536
KVH = 4
HD = 128
GROUP = 3


NEG_BIG = -1e30


def attend_kernel(scal_ref, q_ref, kc_ref, vc_ref, kn_ref, vn_ref, out_ref):
    head = pl.program_id(0) * GROUP + pl.program_id(1)
    heads = KVH * GROUP
    ctx_pos = scal_ref[0]
    length = scal_ref[1]
    scale = HD ** (-0.5)
    q = q_ref[...]
    dims = (((1,), (1,)), ((), ()))
    s_c = lax.dot_general(q, kc_ref[...], dims, preferred_element_type=jnp.float32) * scale
    s_n = lax.dot_general(q, kn_ref[...], dims, preferred_element_type=jnp.float32) * scale
    n_q, n_cache = s_c.shape
    n_new = s_n.shape[1]
    use_c = ctx_pos * n_cache + lax.broadcasted_iota(jnp.int32, (n_q, n_cache), 1) < length
    use_n = ctx_pos * n_new + lax.broadcasted_iota(jnp.int32, (n_q, n_new), 1) <= (
        lax.broadcasted_iota(jnp.int32, (n_q, n_new), 0)
    )
    top = jnp.maximum(
        jnp.max(jnp.where(use_c, s_c, NEG_BIG), 1, keepdims=True),
        jnp.max(jnp.where(use_n, s_n, NEG_BIG), 1, keepdims=True),
    )
    p_c = jnp.where(use_c, jnp.exp(s_c - top), 0.0)
    p_n = jnp.where(use_n, jnp.exp(s_n - top), 0.0)
    total = jnp.sum(p_c, 1, keepdims=True) + jnp.sum(p_n, 1, keepdims=True)
    acc = jnp.dot(
        p_c.astype(jnp.bfloat16), vc_ref[...], preferred_element_type=jnp.float32
    ) + jnp.dot(p_n.astype(jnp.bfloat16), vn_ref[...], preferred_element_type=jnp.float32)
    out_ref[:, pl.ds(pl.multiple_of(head * HD, HD), HD)] = acc.astype(out_ref.dtype)
    stat_cols = slice(heads * HD, (heads + 1) * HD)

    @pl.when(head == 0)
    def _():
        out_ref[:, stat_cols] = jnp.zeros((n_q, HD), out_ref.dtype)

    top_hi = top.astype(jnp.bfloat16).astype(jnp.float32)
    total_hi = total.astype(jnp.bfloat16).astype(jnp.float32)
    lane = lax.broadcasted_iota(jnp.int32, (n_q, HD), 1)
    held = out_ref[:, stat_cols].astype(jnp.float32)
    held = jnp.where(lane == head, top_hi, held)
    held = jnp.where(lane == heads + head, top - top_hi, held)
    held = jnp.where(lane == 2 * heads + head, total_hi, held)
    held = jnp.where(lane == 3 * heads + head, total - total_hi, held)
    out_ref[:, stat_cols] = held.astype(out_ref.dtype)


def partial_attention(scal, all_queries, cache_rows, new_rows):
    n_q = all_queries.shape[0]
    n_cache = cache_rows.shape[0]
    n_new = new_rows.shape[0]
    heads = KVH * GROUP
    width = (heads + 1) * HD
    cost = pl.CostEstimate(
        flops=4 * n_q * (n_cache + n_new) * HD * heads,
        transcendentals=n_q * (n_cache + n_new) * heads,
        bytes_accessed=2 * (all_queries.size + cache_rows.size + new_rows.size) + 2 * n_q * width,
    )
    return pl.pallas_call(
        attend_kernel,
        out_shape=jax.ShapeDtypeStruct((n_q, width), jnp.bfloat16),
        grid_spec=pltpu.PrefetchScalarGridSpec(
            num_scalar_prefetch=1,
            grid=(KVH, GROUP),
            in_specs=[
                pl.BlockSpec((n_q, HD), lambda k, g, s: (0, k * GROUP + g)),
                pl.BlockSpec((n_cache, HD), lambda k, g, s: (0, k)),
                pl.BlockSpec((n_cache, HD), lambda k, g, s: (0, KVH + k)),
                pl.BlockSpec((n_new, HD), lambda k, g, s: (0, k)),
                pl.BlockSpec((n_new, HD), lambda k, g, s: (0, KVH + k)),
            ],
            out_specs=pl.BlockSpec((n_q, width), lambda k, g, s: (0, 0)),
        ),
        cost_estimate=cost,
    )(scal, all_queries, cache_rows, cache_rows, new_rows, new_rows)


EXP_AXES = ("z", "x", "core")
CHIP_AXES = ("z", "x")


def local(
    residual_in,
    queries,
    new_kv,
    cache_kv,
    cache_len,
    out_proj,
    norm_gain,
    routes,
    route_w,
    w_gate_up,
    w_down,
):
    tok_count = residual_in.shape[1]
    cache_rows = cache_kv.shape[1]
    n_ctx = lax.axis_size("ctx")
    ctx_pos = lax.axis_index("ctx")
    length = cache_len[0]
    score_scale = HD ** (-0.5)
    heads = KVH * GROUP

    top_count = routes.shape[2]
    core_size = lax.axis_size("core")
    core_pos = lax.axis_index("core")
    expert_total = w_gate_up.shape[0] * lax.axis_size(EXP_AXES)
    capacity = min(tok_count, 3 * tok_count * top_count // (2 * expert_total))
    packed = jnp.concatenate(
        [
            routes[0].astype(jnp.bfloat16),
            route_w[0],
            jnp.zeros((tok_count, HD - 2 * top_count), jnp.bfloat16),
        ],
        -1,
    )
    both = lax.all_gather(packed, "core", axis=0, tiled=True)
    routes_both = both[:, :top_count].astype(jnp.int32)
    weights_both = both[:, top_count : 2 * top_count]
    expert_ids = routes_both.reshape(core_size, tok_count * top_count)
    pairs = expert_ids[:, :, None] == expert_ids[:, None, :]
    earlier = jnp.arange(tok_count * top_count)
    earlier = earlier[None, :] < earlier[:, None]
    slot_index = jnp.sum((pairs & earlier[None]).astype(jnp.int32), -1)
    block_rows = core_size * capacity
    source_core = jnp.arange(core_size)[:, None]
    dest = jnp.where(
        expert_ids % core_size == core_pos,
        ((expert_ids // core_size) * capacity + slot_index) * core_size + source_core,
        -1,
    ).reshape(core_size * tok_count, top_count)

    all_queries = lax.all_gather(queries[0], "ctx", axis=0, tiled=True)
    scal = jnp.stack([ctx_pos, length]).astype(jnp.int32)
    part = partial_attention(scal, all_queries, cache_kv[0], new_kv[0])
    got = lax.all_to_all(
        part.reshape(n_ctx, tok_count, part.shape[1]), "ctx", split_axis=0, concat_axis=0, tiled=True
    )
    got_acc = got[..., : heads * HD].astype(jnp.float32).reshape(n_ctx, tok_count, heads, HD)
    got_stats = got[..., heads * HD : heads * HD + 4 * heads].astype(jnp.float32)
    got_stats = got_stats.reshape(n_ctx, tok_count, 4, heads)
    got_max = got_stats[:, :, 0] + got_stats[:, :, 1]
    got_sum = got_stats[:, :, 2] + got_stats[:, :, 3]
    top_max = jnp.max(got_max, 0)
    rescale = jnp.exp(got_max - top_max[None])
    total_sum = jnp.sum(rescale * got_sum, 0)
    total_acc = jnp.sum(rescale[..., None] * got_acc, 0)
    attended = (total_acc / total_sum[..., None]).reshape(tok_count, heads * HD)
    attended = attended.astype(jnp.bfloat16)
    mixed = (
        residual_in[0].astype(jnp.float32)
        + jnp.dot(attended, out_proj, preferred_element_type=jnp.float32)
    ).astype(jnp.bfloat16)
    widened = mixed.astype(jnp.float32)
    normed = (
        widened * lax.rsqrt(jnp.mean(widened * widened, -1, keepdims=True) + 1e-06) * norm_gain
    ).astype(jnp.bfloat16)

    normed_both = lax.all_gather(normed, "core", axis=0, tiled=True)
    chip_count = expert_total // core_size
    slot_ids = jnp.arange(chip_count * block_rows)
    hits = dest[None, :, :] == slot_ids[:, None, None]
    slot_shape = (chip_count, capacity, core_size)
    select = jnp.any(hits, -1).astype(jnp.bfloat16).reshape(*slot_shape, -1)
    outgoing = jnp.einsum(
        "jscr,rd->jscd", select, normed_both, preferred_element_type=jnp.float32
    ).astype(jnp.bfloat16)
    incoming = lax.all_to_all(outgoing, CHIP_AXES, split_axis=0, concat_axis=0, tiled=True)
    hidden_half = w_gate_up.shape[2] // 2
    gate_up = jnp.einsum("jscd,df->jscf", incoming, w_gate_up[0], preferred_element_type=jnp.float32)
    activated = (jax.nn.silu(gate_up[..., :hidden_half]) * gate_up[..., hidden_half:]).astype(
        jnp.bfloat16
    )
    result = jnp.einsum(
        "jscf,fd->jscd", activated, w_down[0], preferred_element_type=jnp.float32
    ).astype(jnp.bfloat16)
    returned = lax.all_to_all(result, CHIP_AXES, split_axis=0, concat_axis=0, tiled=True)
    combine = jnp.sum(
        jnp.where(
            hits.transpose(1, 0, 2), weights_both[:, None, :], jnp.zeros((), weights_both.dtype)
        ),
        -1,
    ).reshape(-1, *slot_shape)
    partial = jnp.einsum("tjsc,jscd->td", combine, returned, preferred_element_type=jnp.float32)
    mine = lax.dynamic_slice_in_dim(partial, core_pos * tok_count, tok_count, 0)
    theirs = lax.dynamic_slice_in_dim(partial, (1 - core_pos) * tok_count, tok_count, 0)
    blended = mine + lax.ppermute(theirs, "core", [(0, 1), (1, 0)])
    return (widened + blended).astype(jnp.bfloat16)[None]


def solution(mesh):
    exp_size = mesh.shape["exp"]
    x_size, core_size = 4, 2
    devices = mesh.devices.reshape(
        mesh.shape["ctx"], exp_size // (x_size * core_size), x_size, core_size
    )
    fine = Mesh(devices, ("ctx",) + EXP_AXES)
    rows = P(EXP_AXES, "ctx", None)
    return jax.shard_map(
        local,
        mesh=fine,
        in_specs=(
            rows,
            rows,
            rows,
            rows,
            P(EXP_AXES),
            P(),
            P(),
            rows,
            rows,
            P(EXP_AXES, None, None),
            P(EXP_AXES, None, None),
        ),
        out_specs=rows,
        check_vma=False,
    )
```

```python
import jax
import jax.numpy as jnp
from jax import lax
from jax.experimental import pallas as pl
from jax.experimental.pallas import tpu as pltpu
from jax.sharding import Mesh, PartitionSpec as P

D = 1536
KVH = 4
HD = 128
GROUP = 3


NEG_BIG = -1e30


def attend_kernel(scal_ref, q_ref, kc_ref, vc_ref, kn_ref, vn_ref, out_ref):
    head = pl.program_id(0) * GROUP + pl.program_id(1)
    heads = KVH * GROUP
    ctx_pos = scal_ref[0]
    length = scal_ref[1]
    scale = HD ** (-0.5)
    q = q_ref[...]
    dims = (((1,), (1,)), ((), ()))
    s_c = lax.dot_general(q, kc_ref[...], dims, preferred_element_type=jnp.float32) * scale
    s_n = lax.dot_general(q, kn_ref[...], dims, preferred_element_type=jnp.float32) * scale
    n_q, n_cache = s_c.shape
    n_new = s_n.shape[1]
    use_c = ctx_pos * n_cache + lax.broadcasted_iota(jnp.int32, (n_q, n_cache), 1) < length
    use_n = ctx_pos * n_new + lax.broadcasted_iota(jnp.int32, (n_q, n_new), 1) <= (
        lax.broadcasted_iota(jnp.int32, (n_q, n_new), 0)
    )
    top = jnp.maximum(
        jnp.max(jnp.where(use_c, s_c, NEG_BIG), 1, keepdims=True),
        jnp.max(jnp.where(use_n, s_n, NEG_BIG), 1, keepdims=True),
    )
    p_c = jnp.where(use_c, jnp.exp(s_c - top), 0.0)
    p_n = jnp.where(use_n, jnp.exp(s_n - top), 0.0)
    total = jnp.sum(p_c, 1, keepdims=True) + jnp.sum(p_n, 1, keepdims=True)
    acc = jnp.dot(
        p_c.astype(jnp.bfloat16), vc_ref[...], preferred_element_type=jnp.float32
    ) + jnp.dot(p_n.astype(jnp.bfloat16), vn_ref[...], preferred_element_type=jnp.float32)
    out_ref[:, pl.ds(pl.multiple_of(head * HD, HD), HD)] = acc.astype(out_ref.dtype)
    stat_cols = slice(heads * HD, (heads + 1) * HD)

    @pl.when(head == 0)
    def _():
        out_ref[:, stat_cols] = jnp.zeros((n_q, HD), out_ref.dtype)

    top_hi = top.astype(jnp.bfloat16).astype(jnp.float32)
    total_hi = total.astype(jnp.bfloat16).astype(jnp.float32)
    lane = lax.broadcasted_iota(jnp.int32, (n_q, HD), 1)
    held = out_ref[:, stat_cols].astype(jnp.float32)
    held = jnp.where(lane == head, top_hi, held)
    held = jnp.where(lane == heads + head, top - top_hi, held)
    held = jnp.where(lane == 2 * heads + head, total_hi, held)
    held = jnp.where(lane == 3 * heads + head, total - total_hi, held)
    out_ref[:, stat_cols] = held.astype(out_ref.dtype)


def partial_attention(scal, all_queries, cache_rows, new_rows):
    n_q = all_queries.shape[0]
    n_cache = cache_rows.shape[0]
    n_new = new_rows.shape[0]
    heads = KVH * GROUP
    width = (heads + 1) * HD
    cost = pl.CostEstimate(
        flops=4 * n_q * (n_cache + n_new) * HD * heads,
        transcendentals=n_q * (n_cache + n_new) * heads,
        bytes_accessed=2 * (all_queries.size + cache_rows.size + new_rows.size) + 2 * n_q * width,
    )
    return pl.pallas_call(
        attend_kernel,
        out_shape=jax.ShapeDtypeStruct((n_q, width), jnp.bfloat16),
        grid_spec=pltpu.PrefetchScalarGridSpec(
            num_scalar_prefetch=1,
            grid=(KVH, GROUP),
            in_specs=[
                pl.BlockSpec((n_q, HD), lambda k, g, s: (0, k * GROUP + g)),
                pl.BlockSpec((n_cache, HD), lambda k, g, s: (0, k)),
                pl.BlockSpec((n_cache, HD), lambda k, g, s: (0, KVH + k)),
                pl.BlockSpec((n_new, HD), lambda k, g, s: (0, k)),
                pl.BlockSpec((n_new, HD), lambda k, g, s: (0, KVH + k)),
            ],
            out_specs=pl.BlockSpec((n_q, width), lambda k, g, s: (0, 0)),
        ),
        cost_estimate=cost,
    )(scal, all_queries, cache_rows, cache_rows, new_rows, new_rows)


def combine_kernel(got_ref, res_ref, w_ref, gain_ref, mixed_ref, normed_ref):
    heads = KVH * GROUP
    n_src = got_ref.shape[0]
    base = heads * HD
    stats = [got_ref[j, :, base : base + HD].astype(jnp.float32) for j in range(n_src)]
    tops = [st + pltpu.roll(st, HD - heads, 1) for st in stats]
    sums = [pltpu.roll(st, HD - 2 * heads, 1) + pltpu.roll(st, HD - 3 * heads, 1) for st in stats]
    top = tops[0]
    for t in tops[1:]:
        top = jnp.maximum(top, t)
    weights = [jnp.exp(t - top) for t in tops]
    total = weights[0] * sums[0]
    for w, s in zip(weights[1:], sums[1:]):
        total = total + w * s
    scales = [w / total for w in weights]
    cols = []
    for h in range(heads):
        col = scales[0][:, h : h + 1] * got_ref[0, :, h * HD : (h + 1) * HD].astype(jnp.float32)
        for j in range(1, n_src):
            col = col + scales[j][:, h : h + 1] * got_ref[j, :, h * HD : (h + 1) * HD].astype(
                jnp.float32
            )
        cols.append(col.astype(jnp.bfloat16))
    attended = jnp.concatenate(cols, 1)
    mixed = (
        res_ref[...].astype(jnp.float32)
        + jnp.dot(attended, w_ref[...], preferred_element_type=jnp.float32)
    ).astype(jnp.bfloat16)
    mixed_ref[...] = mixed
    wide = mixed.astype(jnp.float32)
    normed = wide * lax.rsqrt(jnp.mean(wide * wide, -1, keepdims=True) + 1e-06) * gain_ref[...]
    normed_ref[...] = normed.astype(jnp.bfloat16)


def combine_and_norm(got, residual, out_proj, norm_gain):
    rows, width = residual.shape
    out = jax.ShapeDtypeStruct((rows, width), jnp.bfloat16)
    cost = pl.CostEstimate(
        flops=2 * rows * out_proj.shape[0] * width,
        transcendentals=0,
        bytes_accessed=2 * (got.size + out_proj.size + 3 * residual.size),
    )
    return pl.pallas_call(
        combine_kernel,
        out_shape=(out, out),
        cost_estimate=cost,
    )(got, residual, out_proj, norm_gain.reshape(1, -1))


EXP_AXES = ("z", "x", "core")
CHIP_AXES = ("z", "x")


def local(
    residual_in,
    queries,
    new_kv,
    cache_kv,
    cache_len,
    out_proj,
    norm_gain,
    routes,
    route_w,
    w_gate_up,
    w_down,
):
    tok_count = residual_in.shape[1]
    cache_rows = cache_kv.shape[1]
    n_ctx = lax.axis_size("ctx")
    ctx_pos = lax.axis_index("ctx")
    length = cache_len[0]
    score_scale = HD ** (-0.5)
    heads = KVH * GROUP

    top_count = routes.shape[2]
    core_size = lax.axis_size("core")
    core_pos = lax.axis_index("core")
    expert_total = w_gate_up.shape[0] * lax.axis_size(EXP_AXES)
    capacity = min(tok_count, 3 * tok_count * top_count // (2 * expert_total))
    packed = jnp.concatenate(
        [
            routes[0].astype(jnp.bfloat16),
            route_w[0],
            jnp.zeros((tok_count, HD - 2 * top_count), jnp.bfloat16),
        ],
        -1,
    )
    both = lax.all_gather(packed, "core", axis=0, tiled=True)
    routes_both = both[:, :top_count].astype(jnp.int32)
    weights_both = both[:, top_count : 2 * top_count]
    expert_ids = routes_both.reshape(core_size, tok_count * top_count)
    pairs = expert_ids[:, :, None] == expert_ids[:, None, :]
    earlier = jnp.arange(tok_count * top_count)
    earlier = earlier[None, :] < earlier[:, None]
    slot_index = jnp.sum((pairs & earlier[None]).astype(jnp.int32), -1)
    block_rows = core_size * capacity
    source_core = jnp.arange(core_size)[:, None]
    dest = jnp.where(
        expert_ids % core_size == core_pos,
        ((expert_ids // core_size) * capacity + slot_index) * core_size + source_core,
        -1,
    ).reshape(core_size * tok_count, top_count)

    all_queries = lax.all_gather(queries[0], "ctx", axis=0, tiled=True)
    scal = jnp.stack([ctx_pos, length]).astype(jnp.int32)
    part = partial_attention(scal, all_queries, cache_kv[0], new_kv[0])
    got = lax.all_to_all(
        part.reshape(n_ctx, tok_count, part.shape[1]), "ctx", split_axis=0, concat_axis=0, tiled=True
    )
    mixed, normed = combine_and_norm(got, residual_in[0], out_proj, norm_gain)
    widened = mixed.astype(jnp.float32)

    normed_both = lax.all_gather(normed, "core", axis=0, tiled=True)
    chip_count = expert_total // core_size
    slot_ids = jnp.arange(chip_count * block_rows)
    hits = dest[None, :, :] == slot_ids[:, None, None]
    slot_shape = (chip_count, capacity, core_size)
    select = jnp.any(hits, -1).astype(jnp.bfloat16).reshape(*slot_shape, -1)
    outgoing = jnp.einsum(
        "jscr,rd->jscd", select, normed_both, preferred_element_type=jnp.float32
    ).astype(jnp.bfloat16)
    incoming = lax.all_to_all(outgoing, CHIP_AXES, split_axis=0, concat_axis=0, tiled=True)
    hidden_half = w_gate_up.shape[2] // 2
    gate_up = jnp.einsum("jscd,df->jscf", incoming, w_gate_up[0], preferred_element_type=jnp.float32)
    activated = (jax.nn.silu(gate_up[..., :hidden_half]) * gate_up[..., hidden_half:]).astype(
        jnp.bfloat16
    )
    result = jnp.einsum(
        "jscf,fd->jscd", activated, w_down[0], preferred_element_type=jnp.float32
    ).astype(jnp.bfloat16)
    returned = lax.all_to_all(result, CHIP_AXES, split_axis=0, concat_axis=0, tiled=True)
    combine = jnp.sum(
        jnp.where(
            hits.transpose(1, 0, 2), weights_both[:, None, :], jnp.zeros((), weights_both.dtype)
        ),
        -1,
    ).reshape(-1, *slot_shape)
    partial = jnp.einsum("tjsc,jscd->td", combine, returned, preferred_element_type=jnp.float32)
    mine = lax.dynamic_slice_in_dim(partial, core_pos * tok_count, tok_count, 0)
    theirs = lax.dynamic_slice_in_dim(partial, (1 - core_pos) * tok_count, tok_count, 0)
    blended = mine + lax.ppermute(theirs, "core", [(0, 1), (1, 0)])
    return (widened + blended).astype(jnp.bfloat16)[None]


def solution(mesh):
    exp_size = mesh.shape["exp"]
    x_size, core_size = 4, 2
    devices = mesh.devices.reshape(
        mesh.shape["ctx"], exp_size // (x_size * core_size), x_size, core_size
    )
    fine = Mesh(devices, ("ctx",) + EXP_AXES)
    rows = P(EXP_AXES, "ctx", None)
    return jax.shard_map(
        local,
        mesh=fine,
        in_specs=(
            rows,
            rows,
            rows,
            rows,
            P(EXP_AXES),
            P(),
            P(),
            rows,
            rows,
            P(EXP_AXES, None, None),
            P(EXP_AXES, None, None),
        ),
        out_specs=rows,
        check_vma=False,
    )
```

```python
import jax
import jax.numpy as jnp
from jax import lax
from jax.experimental import pallas as pl
from jax.experimental.pallas import tpu as pltpu
from jax.sharding import Mesh, PartitionSpec as P

D = 1536
KVH = 4
HD = 128
GROUP = 3


NEG_BIG = -1e30


def attend_kernel(scal_ref, q_ref, kc_ref, vc_ref, kn_ref, vn_ref, out_ref):
    head = pl.program_id(0) * GROUP + pl.program_id(1)
    heads = KVH * GROUP
    ctx_pos = scal_ref[0]
    length = scal_ref[1]
    scale = HD ** (-0.5)
    q = q_ref[...]
    dims = (((1,), (1,)), ((), ()))
    s_c = lax.dot_general(q, kc_ref[...], dims, preferred_element_type=jnp.float32) * scale
    s_n = lax.dot_general(q, kn_ref[...], dims, preferred_element_type=jnp.float32) * scale
    n_q, n_cache = s_c.shape
    n_new = s_n.shape[1]
    use_c = ctx_pos * n_cache + lax.broadcasted_iota(jnp.int32, (n_q, n_cache), 1) < length
    use_n = ctx_pos * n_new + lax.broadcasted_iota(jnp.int32, (n_q, n_new), 1) <= (
        lax.broadcasted_iota(jnp.int32, (n_q, n_new), 0)
    )
    top = jnp.maximum(
        jnp.max(jnp.where(use_c, s_c, NEG_BIG), 1, keepdims=True),
        jnp.max(jnp.where(use_n, s_n, NEG_BIG), 1, keepdims=True),
    )
    p_c = jnp.where(use_c, jnp.exp(s_c - top), 0.0)
    p_n = jnp.where(use_n, jnp.exp(s_n - top), 0.0)
    total = jnp.sum(p_c, 1, keepdims=True) + jnp.sum(p_n, 1, keepdims=True)
    acc = jnp.dot(
        p_c.astype(jnp.bfloat16), vc_ref[...], preferred_element_type=jnp.float32
    ) + jnp.dot(p_n.astype(jnp.bfloat16), vn_ref[...], preferred_element_type=jnp.float32)
    out_ref[:, pl.ds(pl.multiple_of(head * HD, HD), HD)] = acc.astype(out_ref.dtype)
    stat_cols = slice(heads * HD, (heads + 1) * HD)

    @pl.when(head == 0)
    def _():
        out_ref[:, stat_cols] = jnp.zeros((n_q, HD), out_ref.dtype)

    top_hi = top.astype(jnp.bfloat16).astype(jnp.float32)
    total_hi = total.astype(jnp.bfloat16).astype(jnp.float32)
    lane = lax.broadcasted_iota(jnp.int32, (n_q, HD), 1)
    held = out_ref[:, stat_cols].astype(jnp.float32)
    held = jnp.where(lane == head, top_hi, held)
    held = jnp.where(lane == heads + head, top - top_hi, held)
    held = jnp.where(lane == 2 * heads + head, total_hi, held)
    held = jnp.where(lane == 3 * heads + head, total - total_hi, held)
    out_ref[:, stat_cols] = held.astype(out_ref.dtype)


def partial_attention(scal, all_queries, cache_rows, new_rows):
    n_q = all_queries.shape[0]
    n_cache = cache_rows.shape[0]
    n_new = new_rows.shape[0]
    heads = KVH * GROUP
    width = (heads + 1) * HD
    cost = pl.CostEstimate(
        flops=4 * n_q * (n_cache + n_new) * HD * heads,
        transcendentals=n_q * (n_cache + n_new) * heads,
        bytes_accessed=2 * (all_queries.size + cache_rows.size + new_rows.size) + 2 * n_q * width,
    )
    return pl.pallas_call(
        attend_kernel,
        out_shape=jax.ShapeDtypeStruct((n_q, width), jnp.bfloat16),
        grid_spec=pltpu.PrefetchScalarGridSpec(
            num_scalar_prefetch=1,
            grid=(KVH, GROUP),
            in_specs=[
                pl.BlockSpec((n_q, HD), lambda k, g, s: (0, k * GROUP + g)),
                pl.BlockSpec((n_cache, HD), lambda k, g, s: (0, k)),
                pl.BlockSpec((n_cache, HD), lambda k, g, s: (0, KVH + k)),
                pl.BlockSpec((n_new, HD), lambda k, g, s: (0, k)),
                pl.BlockSpec((n_new, HD), lambda k, g, s: (0, KVH + k)),
            ],
            out_specs=pl.BlockSpec((n_q, width), lambda k, g, s: (0, 0)),
        ),
        cost_estimate=cost,
    )(scal, all_queries, cache_rows, cache_rows, new_rows, new_rows)


def combine_kernel(got_ref, res_ref, w_ref, gain_ref, mixed_ref, normed_ref):
    heads = KVH * GROUP
    n_src = got_ref.shape[0]
    base = heads * HD
    stats = [got_ref[j, :, base : base + HD].astype(jnp.float32) for j in range(n_src)]
    tops = [st + pltpu.roll(st, HD - heads, 1) for st in stats]
    sums = [pltpu.roll(st, HD - 2 * heads, 1) + pltpu.roll(st, HD - 3 * heads, 1) for st in stats]
    top = tops[0]
    for t in tops[1:]:
        top = jnp.maximum(top, t)
    weights = [jnp.exp(t - top) for t in tops]
    total = weights[0] * sums[0]
    for w, s in zip(weights[1:], sums[1:]):
        total = total + w * s
    inverse = 1.0 / total
    inverse = inverse * (2.0 - total * inverse)
    scales = [w * inverse for w in weights]
    cols = []
    for h in range(heads):
        col = scales[0][:, h : h + 1] * got_ref[0, :, h * HD : (h + 1) * HD].astype(jnp.float32)
        for j in range(1, n_src):
            col = col + scales[j][:, h : h + 1] * got_ref[j, :, h * HD : (h + 1) * HD].astype(
                jnp.float32
            )
        cols.append(col.astype(jnp.bfloat16))
    attended = jnp.concatenate(cols, 1)
    mixed = (
        res_ref[...].astype(jnp.float32)
        + jnp.dot(attended, w_ref[...], preferred_element_type=jnp.float32)
    ).astype(jnp.bfloat16)
    mixed_ref[...] = mixed
    wide = mixed.astype(jnp.float32)
    square_mean = jnp.mean(wide * wide, -1, keepdims=True) + 1e-06
    root = lax.rsqrt(square_mean)
    root = root * (1.5 - 0.5 * square_mean * root * root)
    normed = wide * root * gain_ref[...]
    normed_ref[...] = normed.astype(jnp.bfloat16)


def combine_and_norm(got, residual, out_proj, norm_gain):
    rows, width = residual.shape
    out = jax.ShapeDtypeStruct((rows, width), jnp.bfloat16)
    cost = pl.CostEstimate(
        flops=2 * rows * out_proj.shape[0] * width,
        transcendentals=0,
        bytes_accessed=2 * (got.size + out_proj.size + 3 * residual.size),
    )
    return pl.pallas_call(
        combine_kernel,
        out_shape=(out, out),
        cost_estimate=cost,
    )(got, residual, out_proj, norm_gain.reshape(1, -1))


EXP_AXES = ("z", "x", "core")
CHIP_AXES = ("z", "x")


def local(
    residual_in,
    queries,
    new_kv,
    cache_kv,
    cache_len,
    out_proj,
    norm_gain,
    routes,
    route_w,
    w_gate_up,
    w_down,
):
    tok_count = residual_in.shape[1]
    cache_rows = cache_kv.shape[1]
    n_ctx = lax.axis_size("ctx")
    ctx_pos = lax.axis_index("ctx")
    length = cache_len[0]
    score_scale = HD ** (-0.5)
    heads = KVH * GROUP

    top_count = routes.shape[2]
    core_size = lax.axis_size("core")
    core_pos = lax.axis_index("core")
    expert_total = w_gate_up.shape[0] * lax.axis_size(EXP_AXES)
    capacity = min(tok_count, 3 * tok_count * top_count // (2 * expert_total))
    packed = jnp.concatenate(
        [
            routes[0].astype(jnp.bfloat16),
            route_w[0],
            jnp.zeros((tok_count, HD - 2 * top_count), jnp.bfloat16),
        ],
        -1,
    )
    both = lax.all_gather(packed, "core", axis=0, tiled=True)
    routes_both = both[:, :top_count].astype(jnp.int32)
    weights_both = both[:, top_count : 2 * top_count]
    expert_ids = routes_both.reshape(core_size, tok_count * top_count)
    pairs = expert_ids[:, :, None] == expert_ids[:, None, :]
    earlier = jnp.arange(tok_count * top_count)
    earlier = earlier[None, :] < earlier[:, None]
    slot_index = jnp.sum((pairs & earlier[None]).astype(jnp.int32), -1)
    block_rows = core_size * capacity
    source_core = jnp.arange(core_size)[:, None]
    dest = jnp.where(
        expert_ids % core_size == core_pos,
        ((expert_ids // core_size) * capacity + slot_index) * core_size + source_core,
        -1,
    ).reshape(core_size * tok_count, top_count)

    all_queries = lax.all_gather(queries[0], "ctx", axis=0, tiled=True)
    scal = jnp.stack([ctx_pos, length]).astype(jnp.int32)
    part = partial_attention(scal, all_queries, cache_kv[0], new_kv[0])
    got = lax.all_to_all(
        part.reshape(n_ctx, tok_count, part.shape[1]), "ctx", split_axis=0, concat_axis=0, tiled=True
    )
    mixed, normed = combine_and_norm(got, residual_in[0], out_proj, norm_gain)
    widened = mixed.astype(jnp.float32)

    normed_both = lax.all_gather(normed, "core", axis=0, tiled=True)
    chip_count = expert_total // core_size
    slot_ids = jnp.arange(chip_count * block_rows)
    hits = dest[None, :, :] == slot_ids[:, None, None]
    slot_shape = (chip_count, capacity, core_size)
    select = jnp.any(hits, -1).astype(jnp.bfloat16).reshape(*slot_shape, -1)
    outgoing = jnp.einsum(
        "jscr,rd->jscd", select, normed_both, preferred_element_type=jnp.float32
    ).astype(jnp.bfloat16)
    incoming = lax.all_to_all(outgoing, CHIP_AXES, split_axis=0, concat_axis=0, tiled=True)
    hidden_half = w_gate_up.shape[2] // 2
    gate_up = jnp.einsum("jscd,df->jscf", incoming, w_gate_up[0], preferred_element_type=jnp.float32)
    activated = (jax.nn.silu(gate_up[..., :hidden_half]) * gate_up[..., hidden_half:]).astype(
        jnp.bfloat16
    )
    result = jnp.einsum(
        "jscf,fd->jscd", activated, w_down[0], preferred_element_type=jnp.float32
    ).astype(jnp.bfloat16)
    returned = lax.all_to_all(result, CHIP_AXES, split_axis=0, concat_axis=0, tiled=True)
    combine = jnp.sum(
        jnp.where(
            hits.transpose(1, 0, 2), weights_both[:, None, :], jnp.zeros((), weights_both.dtype)
        ),
        -1,
    ).reshape(core_size, tok_count, *slot_shape)
    theirs = jnp.einsum(
        "tjsc,jscd->td", combine[1 - core_pos], returned, preferred_element_type=jnp.float32
    )
    sent = lax.ppermute(theirs, "core", [(0, 1), (1, 0)])
    mine = jnp.einsum(
        "tjsc,jscd->td", combine[core_pos], returned, preferred_element_type=jnp.float32
    )
    blended = lax.optimization_barrier(mine) + sent
    return (widened + blended).astype(jnp.bfloat16)[None]


def solution(mesh):
    exp_size = mesh.shape["exp"]
    x_size, core_size = 4, 2
    devices = mesh.devices.reshape(
        mesh.shape["ctx"], exp_size // (x_size * core_size), x_size, core_size
    )
    fine = Mesh(devices, ("ctx",) + EXP_AXES)
    rows = P(EXP_AXES, "ctx", None)
    return jax.shard_map(
        local,
        mesh=fine,
        in_specs=(
            rows,
            rows,
            rows,
            rows,
            P(EXP_AXES),
            P(),
            P(),
            rows,
            rows,
            P(EXP_AXES, None, None),
            P(EXP_AXES, None, None),
        ),
        out_specs=rows,
        check_vma=False,
    )
```

```python
import jax
import jax.numpy as jnp
from jax import lax
from jax.experimental import pallas as pl
from jax.experimental.pallas import tpu as pltpu
from jax.sharding import Mesh, PartitionSpec as P

D = 1536
KVH = 4
HD = 128
GROUP = 3


NEG_BIG = -1e30


def attend_kernel(scal_ref, q_ref, kc_ref, vc_ref, kn_ref, vn_ref, out_ref):
    head = pl.program_id(0) * GROUP + pl.program_id(1)
    heads = KVH * GROUP
    ctx_pos = scal_ref[0]
    length = scal_ref[1]
    scale = HD ** (-0.5)
    q = q_ref[...]
    dims = (((1,), (1,)), ((), ()))
    s_c = lax.dot_general(q, kc_ref[...], dims, preferred_element_type=jnp.float32) * scale
    s_n = lax.dot_general(q, kn_ref[...], dims, preferred_element_type=jnp.float32) * scale
    n_q, n_cache = s_c.shape
    n_new = s_n.shape[1]
    use_c = lax.broadcasted_iota(jnp.int32, (n_q, n_cache), 1) < length - ctx_pos * n_cache
    use_n = ctx_pos * n_new + lax.broadcasted_iota(jnp.int32, (n_q, n_new), 1) <= (
        lax.broadcasted_iota(jnp.int32, (n_q, n_new), 0)
    )
    s_c = jnp.where(use_c, s_c, NEG_BIG)
    s_n = jnp.where(use_n, s_n, NEG_BIG)
    top = jnp.maximum(
        jnp.maximum(jnp.max(s_c, 1, keepdims=True), jnp.max(s_n, 1, keepdims=True)),
        NEG_BIG / 10,
    )
    p_c = jnp.exp(s_c - top)
    p_n = jnp.exp(s_n - top)
    total = jnp.sum(p_c, 1, keepdims=True) + jnp.sum(p_n, 1, keepdims=True)
    acc = jnp.dot(
        p_c.astype(jnp.bfloat16), vc_ref[...], preferred_element_type=jnp.float32
    ) + jnp.dot(p_n.astype(jnp.bfloat16), vn_ref[...], preferred_element_type=jnp.float32)
    out_ref[:, pl.ds(pl.multiple_of(head * HD, HD), HD)] = acc.astype(out_ref.dtype)
    stat_cols = slice(heads * HD, (heads + 1) * HD)

    @pl.when(head == 0)
    def _():
        out_ref[:, stat_cols] = jnp.zeros((n_q, HD), out_ref.dtype)

    top_hi = top.astype(jnp.bfloat16).astype(jnp.float32)
    total_hi = total.astype(jnp.bfloat16).astype(jnp.float32)
    lane = lax.broadcasted_iota(jnp.int32, (n_q, HD), 1)
    held = out_ref[:, stat_cols].astype(jnp.float32)
    held = jnp.where(lane == head, top_hi, held)
    held = jnp.where(lane == heads + head, top - top_hi, held)
    held = jnp.where(lane == 2 * heads + head, total_hi, held)
    held = jnp.where(lane == 3 * heads + head, total - total_hi, held)
    out_ref[:, stat_cols] = held.astype(out_ref.dtype)


def partial_attention(scal, all_queries, cache_rows, new_rows):
    n_q = all_queries.shape[0]
    n_cache = cache_rows.shape[0]
    n_new = new_rows.shape[0]
    heads = KVH * GROUP
    width = (heads + 1) * HD
    cost = pl.CostEstimate(
        flops=4 * n_q * (n_cache + n_new) * HD * heads,
        transcendentals=n_q * (n_cache + n_new) * heads,
        bytes_accessed=2 * (all_queries.size + cache_rows.size + new_rows.size) + 2 * n_q * width,
    )
    return pl.pallas_call(
        attend_kernel,
        out_shape=jax.ShapeDtypeStruct((n_q, width), jnp.bfloat16),
        grid_spec=pltpu.PrefetchScalarGridSpec(
            num_scalar_prefetch=1,
            grid=(KVH, GROUP),
            in_specs=[
                pl.BlockSpec((n_q, HD), lambda k, g, s: (0, k * GROUP + g)),
                pl.BlockSpec((n_cache, HD), lambda k, g, s: (0, k)),
                pl.BlockSpec((n_cache, HD), lambda k, g, s: (0, KVH + k)),
                pl.BlockSpec((n_new, HD), lambda k, g, s: (0, k)),
                pl.BlockSpec((n_new, HD), lambda k, g, s: (0, KVH + k)),
            ],
            out_specs=pl.BlockSpec((n_q, width), lambda k, g, s: (0, 0)),
        ),
        cost_estimate=cost,
    )(scal, all_queries, cache_rows, cache_rows, new_rows, new_rows)


def combine_kernel(got_ref, res_ref, w_ref, gain_ref, mixed_ref, normed_ref):
    heads = KVH * GROUP
    n_src = got_ref.shape[0]
    base = heads * HD
    stats = [got_ref[j, :, base : base + HD].astype(jnp.float32) for j in range(n_src)]
    tops = [st + pltpu.roll(st, HD - heads, 1) for st in stats]
    sums = [pltpu.roll(st, HD - 2 * heads, 1) + pltpu.roll(st, HD - 3 * heads, 1) for st in stats]
    top = tops[0]
    for t in tops[1:]:
        top = jnp.maximum(top, t)
    weights = [jnp.exp(t - top) for t in tops]
    total = weights[0] * sums[0]
    for w, s in zip(weights[1:], sums[1:]):
        total = total + w * s
    inverse = 1.0 / total
    inverse = inverse * (2.0 - total * inverse)
    scales = [w * inverse for w in weights]
    cols = []
    for h in range(heads):
        col = scales[0][:, h : h + 1] * got_ref[0, :, h * HD : (h + 1) * HD].astype(jnp.float32)
        for j in range(1, n_src):
            col = col + scales[j][:, h : h + 1] * got_ref[j, :, h * HD : (h + 1) * HD].astype(
                jnp.float32
            )
        cols.append(col.astype(jnp.bfloat16))
    attended = jnp.concatenate(cols, 1)
    mixed = (
        res_ref[...].astype(jnp.float32)
        + jnp.dot(attended, w_ref[...], preferred_element_type=jnp.float32)
    ).astype(jnp.bfloat16)
    mixed_ref[...] = mixed
    wide = mixed.astype(jnp.float32)
    square_mean = jnp.mean(wide * wide, -1, keepdims=True) + 1e-06
    root = lax.rsqrt(square_mean)
    root = root * (1.5 - 0.5 * square_mean * root * root)
    normed = wide * root * gain_ref[...]
    normed_ref[...] = normed.astype(jnp.bfloat16)


def combine_and_norm(got, residual, out_proj, norm_gain):
    rows, width = residual.shape
    out = jax.ShapeDtypeStruct((rows, width), jnp.bfloat16)
    cost = pl.CostEstimate(
        flops=2 * rows * out_proj.shape[0] * width,
        transcendentals=0,
        bytes_accessed=2 * (got.size + out_proj.size + 3 * residual.size),
    )
    return pl.pallas_call(
        combine_kernel,
        out_shape=(out, out),
        cost_estimate=cost,
    )(got, residual, out_proj, norm_gain.reshape(1, -1))


EXP_AXES = ("z", "x", "core")
CHIP_AXES = ("z", "x")


def local(
    residual_in,
    queries,
    new_kv,
    cache_kv,
    cache_len,
    out_proj,
    norm_gain,
    routes,
    route_w,
    w_gate_up,
    w_down,
):
    tok_count = residual_in.shape[1]
    cache_rows = cache_kv.shape[1]
    n_ctx = lax.axis_size("ctx")
    ctx_pos = lax.axis_index("ctx")
    length = cache_len[0]
    score_scale = HD ** (-0.5)
    heads = KVH * GROUP

    top_count = routes.shape[2]
    core_size = lax.axis_size("core")
    core_pos = lax.axis_index("core")
    expert_total = w_gate_up.shape[0] * lax.axis_size(EXP_AXES)
    capacity = min(tok_count, 3 * tok_count * top_count // (2 * expert_total))
    packed = jnp.concatenate(
        [
            routes[0].astype(jnp.bfloat16),
            route_w[0],
            jnp.zeros((tok_count, HD - 2 * top_count), jnp.bfloat16),
        ],
        -1,
    )
    both = lax.all_gather(packed, "core", axis=0, tiled=True)
    routes_both = both[:, :top_count].astype(jnp.int32)
    weights_both = both[:, top_count : 2 * top_count]
    expert_ids = routes_both.reshape(core_size, tok_count * top_count)
    pairs = expert_ids[:, :, None] == expert_ids[:, None, :]
    earlier = jnp.arange(tok_count * top_count)
    earlier = earlier[None, :] < earlier[:, None]
    slot_index = jnp.sum((pairs & earlier[None]).astype(jnp.int32), -1)
    block_rows = core_size * capacity
    source_core = jnp.arange(core_size)[:, None]
    dest = jnp.where(
        expert_ids % core_size == core_pos,
        ((expert_ids // core_size) * capacity + slot_index) * core_size + source_core,
        -1,
    ).reshape(core_size * tok_count, top_count)

    all_queries = lax.all_gather(queries[0], "ctx", axis=0, tiled=True)
    scal = jnp.stack([ctx_pos, length]).astype(jnp.int32)
    part = partial_attention(scal, all_queries, cache_kv[0], new_kv[0])
    got = lax.all_to_all(
        part.reshape(n_ctx, tok_count, part.shape[1]), "ctx", split_axis=0, concat_axis=0, tiled=True
    )
    mixed, normed = combine_and_norm(got, residual_in[0], out_proj, norm_gain)
    widened = mixed.astype(jnp.float32)

    normed_both = lax.all_gather(normed, "core", axis=0, tiled=True)
    chip_count = expert_total // core_size
    slot_ids = jnp.arange(chip_count * block_rows)
    hits = dest[None, :, :] == slot_ids[:, None, None]
    slot_shape = (chip_count, capacity, core_size)
    select = jnp.any(hits, -1).astype(jnp.bfloat16).reshape(*slot_shape, -1)
    outgoing = jnp.einsum(
        "jscr,rd->jscd", select, normed_both, preferred_element_type=jnp.float32
    ).astype(jnp.bfloat16)
    incoming = lax.all_to_all(outgoing, CHIP_AXES, split_axis=0, concat_axis=0, tiled=True)
    hidden_half = w_gate_up.shape[2] // 2
    gate_up = jnp.einsum("jscd,df->jscf", incoming, w_gate_up[0], preferred_element_type=jnp.float32)
    activated = (jax.nn.silu(gate_up[..., :hidden_half]) * gate_up[..., hidden_half:]).astype(
        jnp.bfloat16
    )
    result = jnp.einsum(
        "jscf,fd->jscd", activated, w_down[0], preferred_element_type=jnp.float32
    ).astype(jnp.bfloat16)
    returned = lax.all_to_all(result, CHIP_AXES, split_axis=0, concat_axis=0, tiled=True)
    combine = jnp.sum(
        jnp.where(
            hits.transpose(1, 0, 2), weights_both[:, None, :], jnp.zeros((), weights_both.dtype)
        ),
        -1,
    ).reshape(core_size, tok_count, *slot_shape)
    theirs = jnp.einsum(
        "tjsc,jscd->td", combine[1 - core_pos], returned, preferred_element_type=jnp.float32
    )
    sent = lax.ppermute(theirs, "core", [(0, 1), (1, 0)])
    mine = jnp.einsum(
        "tjsc,jscd->td", combine[core_pos], returned, preferred_element_type=jnp.float32
    )
    blended = lax.optimization_barrier(mine) + sent
    return (widened + blended).astype(jnp.bfloat16)[None]


def solution(mesh):
    exp_size = mesh.shape["exp"]
    x_size, core_size = 4, 2
    devices = mesh.devices.reshape(
        mesh.shape["ctx"], exp_size // (x_size * core_size), x_size, core_size
    )
    fine = Mesh(devices, ("ctx",) + EXP_AXES)
    rows = P(EXP_AXES, "ctx", None)
    return jax.shard_map(
        local,
        mesh=fine,
        in_specs=(
            rows,
            rows,
            rows,
            rows,
            P(EXP_AXES),
            P(),
            P(),
            rows,
            rows,
            P(EXP_AXES, None, None),
            P(EXP_AXES, None, None),
        ),
        out_specs=rows,
        check_vma=False,
    )
```

```python
import jax
import jax.numpy as jnp
from jax import lax
from jax.experimental import pallas as pl
from jax.experimental.pallas import tpu as pltpu
from jax.sharding import Mesh, PartitionSpec as P

D = 1536
KVH = 4
HD = 128
GROUP = 3


NEG_BIG = -1e30


def attend_kernel(scal_ref, q_ref, kc_ref, vc_ref, kn_ref, vn_ref, out_ref):
    kv_head = pl.program_id(0)
    heads = KVH * GROUP
    ctx_pos = scal_ref[0]
    length = scal_ref[1]
    scale = HD ** (-0.5)
    n_q = q_ref.shape[0]
    q = jnp.concatenate([q_ref[:, g * HD : (g + 1) * HD] for g in range(GROUP)], 0)
    dims = (((1,), (1,)), ((), ()))
    s_c = lax.dot_general(q, kc_ref[...], dims, preferred_element_type=jnp.float32) * scale
    s_n = lax.dot_general(q, kn_ref[...], dims, preferred_element_type=jnp.float32) * scale
    n_rows, n_cache = s_c.shape
    n_new = s_n.shape[1]
    use_c = lax.broadcasted_iota(jnp.int32, (n_rows, n_cache), 1) < length - ctx_pos * n_cache
    causal = ctx_pos * n_new + lax.broadcasted_iota(jnp.int32, (n_q, n_new), 1) <= (
        lax.broadcasted_iota(jnp.int32, (n_q, n_new), 0)
    )
    use_n = jnp.concatenate([causal] * GROUP, 0)
    s_c = jnp.where(use_c, s_c, NEG_BIG)
    s_n = jnp.where(use_n, s_n, NEG_BIG)
    top = jnp.maximum(
        jnp.maximum(jnp.max(s_c, 1, keepdims=True), jnp.max(s_n, 1, keepdims=True)),
        NEG_BIG / 10,
    )
    p_c = jnp.exp(s_c - top)
    p_n = jnp.exp(s_n - top)
    total = jnp.sum(p_c, 1, keepdims=True) + jnp.sum(p_n, 1, keepdims=True)
    acc = jnp.dot(
        p_c.astype(jnp.bfloat16), vc_ref[...], preferred_element_type=jnp.float32
    ) + jnp.dot(p_n.astype(jnp.bfloat16), vn_ref[...], preferred_element_type=jnp.float32)
    stat_cols = slice(heads * HD, (heads + 1) * HD)

    @pl.when(kv_head == 0)
    def _():
        out_ref[:, stat_cols] = jnp.zeros((n_q, HD), out_ref.dtype)

    top_hi = top.astype(jnp.bfloat16).astype(jnp.float32)
    total_hi = total.astype(jnp.bfloat16).astype(jnp.float32)
    lane = lax.broadcasted_iota(jnp.int32, (n_q, HD), 1)
    held = out_ref[:, stat_cols].astype(jnp.float32)
    for g in range(GROUP):
        head = kv_head * GROUP + g
        rows = slice(g * n_q, (g + 1) * n_q)
        out_ref[:, pl.ds(pl.multiple_of(head * HD, HD), HD)] = acc[rows].astype(out_ref.dtype)
        held = jnp.where(lane == head, top_hi[rows], held)
        held = jnp.where(lane == heads + head, (top - top_hi)[rows], held)
        held = jnp.where(lane == 2 * heads + head, total_hi[rows], held)
        held = jnp.where(lane == 3 * heads + head, (total - total_hi)[rows], held)
    out_ref[:, stat_cols] = held.astype(out_ref.dtype)


def partial_attention(scal, all_queries, cache_rows, new_rows):
    n_q = all_queries.shape[0]
    n_cache = cache_rows.shape[0]
    n_new = new_rows.shape[0]
    heads = KVH * GROUP
    width = (heads + 1) * HD
    cost = pl.CostEstimate(
        flops=4 * n_q * (n_cache + n_new) * HD * heads,
        transcendentals=n_q * (n_cache + n_new) * heads,
        bytes_accessed=2 * (all_queries.size + cache_rows.size + new_rows.size) + 2 * n_q * width,
    )
    return pl.pallas_call(
        attend_kernel,
        out_shape=jax.ShapeDtypeStruct((n_q, width), jnp.bfloat16),
        grid_spec=pltpu.PrefetchScalarGridSpec(
            num_scalar_prefetch=1,
            grid=(KVH,),
            in_specs=[
                pl.BlockSpec((n_q, GROUP * HD), lambda k, s: (0, k)),
                pl.BlockSpec((n_cache, HD), lambda k, s: (0, k)),
                pl.BlockSpec((n_cache, HD), lambda k, s: (0, KVH + k)),
                pl.BlockSpec((n_new, HD), lambda k, s: (0, k)),
                pl.BlockSpec((n_new, HD), lambda k, s: (0, KVH + k)),
            ],
            out_specs=pl.BlockSpec((n_q, width), lambda k, s: (0, 0)),
        ),
        cost_estimate=cost,
    )(scal, all_queries, cache_rows, cache_rows, new_rows, new_rows)


def combine_kernel(got_ref, res_ref, w_ref, gain_ref, mixed_ref, normed_ref):
    heads = KVH * GROUP
    n_src = got_ref.shape[0]
    base = heads * HD
    stats = [got_ref[j, :, base : base + HD].astype(jnp.float32) for j in range(n_src)]
    tops = [st + pltpu.roll(st, HD - heads, 1) for st in stats]
    sums = [pltpu.roll(st, HD - 2 * heads, 1) + pltpu.roll(st, HD - 3 * heads, 1) for st in stats]
    top = tops[0]
    for t in tops[1:]:
        top = jnp.maximum(top, t)
    weights = [jnp.exp(t - top) for t in tops]
    total = weights[0] * sums[0]
    for w, s in zip(weights[1:], sums[1:]):
        total = total + w * s
    inverse = 1.0 / total
    inverse = inverse * (2.0 - total * inverse)
    scales = [w * inverse for w in weights]
    cols = []
    for h in range(heads):
        col = scales[0][:, h : h + 1] * got_ref[0, :, h * HD : (h + 1) * HD].astype(jnp.float32)
        for j in range(1, n_src):
            col = col + scales[j][:, h : h + 1] * got_ref[j, :, h * HD : (h + 1) * HD].astype(
                jnp.float32
            )
        cols.append(col.astype(jnp.bfloat16))
    attended = jnp.concatenate(cols, 1)
    mixed = (
        res_ref[...].astype(jnp.float32)
        + jnp.dot(attended, w_ref[...], preferred_element_type=jnp.float32)
    ).astype(jnp.bfloat16)
    mixed_ref[...] = mixed
    wide = mixed.astype(jnp.float32)
    square_mean = jnp.mean(wide * wide, -1, keepdims=True) + 1e-06
    root = lax.rsqrt(square_mean)
    root = root * (1.5 - 0.5 * square_mean * root * root)
    normed = wide * root * gain_ref[...]
    normed_ref[...] = normed.astype(jnp.bfloat16)


def combine_and_norm(got, residual, out_proj, norm_gain):
    rows, width = residual.shape
    out = jax.ShapeDtypeStruct((rows, width), jnp.bfloat16)
    cost = pl.CostEstimate(
        flops=2 * rows * out_proj.shape[0] * width,
        transcendentals=0,
        bytes_accessed=2 * (got.size + out_proj.size + 3 * residual.size),
    )
    return pl.pallas_call(
        combine_kernel,
        out_shape=(out, out),
        cost_estimate=cost,
    )(got, residual, out_proj, norm_gain.reshape(1, -1))


EXP_AXES = ("z", "x", "core")
CHIP_AXES = ("z", "x")


def local(
    residual_in,
    queries,
    new_kv,
    cache_kv,
    cache_len,
    out_proj,
    norm_gain,
    routes,
    route_w,
    w_gate_up,
    w_down,
):
    tok_count = residual_in.shape[1]
    cache_rows = cache_kv.shape[1]
    n_ctx = lax.axis_size("ctx")
    ctx_pos = lax.axis_index("ctx")
    length = cache_len[0]
    score_scale = HD ** (-0.5)
    heads = KVH * GROUP

    top_count = routes.shape[2]
    core_size = lax.axis_size("core")
    core_pos = lax.axis_index("core")
    expert_total = w_gate_up.shape[0] * lax.axis_size(EXP_AXES)
    capacity = min(tok_count, 3 * tok_count * top_count // (2 * expert_total))
    packed = jnp.concatenate(
        [
            routes[0].astype(jnp.bfloat16),
            route_w[0],
            jnp.zeros((tok_count, HD - 2 * top_count), jnp.bfloat16),
        ],
        -1,
    )
    both = lax.all_gather(packed, "core", axis=0, tiled=True)
    routes_both = both[:, :top_count].astype(jnp.int32)
    weights_both = both[:, top_count : 2 * top_count]
    expert_ids = routes_both.reshape(core_size, tok_count * top_count)
    pairs = expert_ids[:, :, None] == expert_ids[:, None, :]
    earlier = jnp.arange(tok_count * top_count)
    earlier = earlier[None, :] < earlier[:, None]
    slot_index = jnp.sum((pairs & earlier[None]).astype(jnp.int32), -1)
    block_rows = core_size * capacity
    source_core = jnp.arange(core_size)[:, None]
    dest = jnp.where(
        expert_ids % core_size == core_pos,
        ((expert_ids // core_size) * capacity + slot_index) * core_size + source_core,
        -1,
    ).reshape(core_size * tok_count, top_count)

    all_queries = lax.all_gather(queries[0], "ctx", axis=0, tiled=True)
    scal = jnp.stack([ctx_pos, length]).astype(jnp.int32)
    part = partial_attention(scal, all_queries, cache_kv[0], new_kv[0])
    got = lax.all_to_all(
        part.reshape(n_ctx, tok_count, part.shape[1]), "ctx", split_axis=0, concat_axis=0, tiled=True
    )
    mixed, normed = combine_and_norm(got, residual_in[0], out_proj, norm_gain)
    widened = mixed.astype(jnp.float32)

    normed_both = lax.all_gather(normed, "core", axis=0, tiled=True)
    chip_count = expert_total // core_size
    slot_ids = jnp.arange(chip_count * block_rows)
    hits = dest[None, :, :] == slot_ids[:, None, None]
    slot_shape = (chip_count, capacity, core_size)
    select = jnp.any(hits, -1).astype(jnp.bfloat16).reshape(*slot_shape, -1)
    outgoing = jnp.einsum(
        "jscr,rd->jscd", select, normed_both, preferred_element_type=jnp.float32
    ).astype(jnp.bfloat16)
    incoming = lax.all_to_all(outgoing, CHIP_AXES, split_axis=0, concat_axis=0, tiled=True)
    hidden_half = w_gate_up.shape[2] // 2
    gate_up = jnp.einsum("jscd,df->jscf", incoming, w_gate_up[0], preferred_element_type=jnp.float32)
    activated = (jax.nn.silu(gate_up[..., :hidden_half]) * gate_up[..., hidden_half:]).astype(
        jnp.bfloat16
    )
    result = jnp.einsum(
        "jscf,fd->jscd", activated, w_down[0], preferred_element_type=jnp.float32
    ).astype(jnp.bfloat16)
    returned = lax.all_to_all(result, CHIP_AXES, split_axis=0, concat_axis=0, tiled=True)
    combine = jnp.sum(
        jnp.where(
            hits.transpose(1, 0, 2), weights_both[:, None, :], jnp.zeros((), weights_both.dtype)
        ),
        -1,
    ).reshape(core_size, tok_count, *slot_shape)
    theirs = jnp.einsum(
        "tjsc,jscd->td", combine[1 - core_pos], returned, preferred_element_type=jnp.float32
    )
    sent = lax.ppermute(theirs, "core", [(0, 1), (1, 0)])
    mine = jnp.einsum(
        "tjsc,jscd->td", combine[core_pos], returned, preferred_element_type=jnp.float32
    )
    blended = lax.optimization_barrier(mine) + sent
    return (widened + blended).astype(jnp.bfloat16)[None]


def solution(mesh):
    exp_size = mesh.shape["exp"]
    x_size, core_size = 4, 2
    devices = mesh.devices.reshape(
        mesh.shape["ctx"], exp_size // (x_size * core_size), x_size, core_size
    )
    fine = Mesh(devices, ("ctx",) + EXP_AXES)
    rows = P(EXP_AXES, "ctx", None)
    return jax.shard_map(
        local,
        mesh=fine,
        in_specs=(
            rows,
            rows,
            rows,
            rows,
            P(EXP_AXES),
            P(),
            P(),
            rows,
            rows,
            P(EXP_AXES, None, None),
            P(EXP_AXES, None, None),
        ),
        out_specs=rows,
        check_vma=False,
    )
```

```python
import jax
import jax.numpy as jnp
from jax import lax
from jax.experimental import pallas as pl
from jax.experimental.pallas import tpu as pltpu
from jax.sharding import Mesh, PartitionSpec as P

D = 1536
KVH = 4
HD = 128
GROUP = 3


NEG_BIG = -1e30


def attend_kernel(scal_ref, q_ref, kc_ref, vc_ref, kn_ref, vn_ref, out_ref):
    kv_head = pl.program_id(0)
    heads = KVH * GROUP
    ctx_pos = scal_ref[0]
    length = scal_ref[1]
    scale = HD ** (-0.5)
    scale_log2 = scale * 1.4426950408889634
    n_q = q_ref.shape[0]
    q = jnp.concatenate([q_ref[:, g * HD : (g + 1) * HD] for g in range(GROUP)], 0)
    dims = (((1,), (1,)), ((), ()))
    s_c = lax.dot_general(q, kc_ref[...], dims, preferred_element_type=jnp.float32)
    s_n = lax.dot_general(q, kn_ref[...], dims, preferred_element_type=jnp.float32)
    n_rows, n_cache = s_c.shape
    n_new = s_n.shape[1]
    use_c = lax.broadcasted_iota(jnp.int32, (n_rows, n_cache), 1) < length - ctx_pos * n_cache
    causal = ctx_pos * n_new + lax.broadcasted_iota(jnp.int32, (n_q, n_new), 1) <= (
        lax.broadcasted_iota(jnp.int32, (n_q, n_new), 0)
    )
    use_n = jnp.concatenate([causal] * GROUP, 0)
    s_c = jnp.where(use_c, s_c, NEG_BIG)
    s_n = jnp.where(use_n, s_n, NEG_BIG)
    top = jnp.maximum(
        jnp.maximum(jnp.max(s_c, 1, keepdims=True), jnp.max(s_n, 1, keepdims=True)),
        NEG_BIG / 10,
    )
    p_c = jnp.exp2((s_c - top) * scale_log2)
    p_n = jnp.exp2((s_n - top) * scale_log2)
    top = top * scale
    total = jnp.sum(p_c, 1, keepdims=True) + jnp.sum(p_n, 1, keepdims=True)
    acc = jnp.dot(
        p_c.astype(jnp.bfloat16), vc_ref[...], preferred_element_type=jnp.float32
    ) + jnp.dot(p_n.astype(jnp.bfloat16), vn_ref[...], preferred_element_type=jnp.float32)
    stat_cols = slice(heads * HD, (heads + 1) * HD)

    @pl.when(kv_head == 0)
    def _():
        out_ref[:, stat_cols] = jnp.zeros((n_q, HD), out_ref.dtype)

    top_hi = top.astype(jnp.bfloat16).astype(jnp.float32)
    total_hi = total.astype(jnp.bfloat16).astype(jnp.float32)
    lane = lax.broadcasted_iota(jnp.int32, (n_q, HD), 1)
    held = out_ref[:, stat_cols].astype(jnp.float32)
    for g in range(GROUP):
        head = kv_head * GROUP + g
        rows = slice(g * n_q, (g + 1) * n_q)
        out_ref[:, pl.ds(pl.multiple_of(head * HD, HD), HD)] = acc[rows].astype(out_ref.dtype)
        held = jnp.where(lane == head, top_hi[rows], held)
        held = jnp.where(lane == heads + head, (top - top_hi)[rows], held)
        held = jnp.where(lane == 2 * heads + head, total_hi[rows], held)
        held = jnp.where(lane == 3 * heads + head, (total - total_hi)[rows], held)
    out_ref[:, stat_cols] = held.astype(out_ref.dtype)


def partial_attention(scal, all_queries, cache_rows, new_rows):
    n_q = all_queries.shape[0]
    n_cache = cache_rows.shape[0]
    n_new = new_rows.shape[0]
    heads = KVH * GROUP
    width = (heads + 1) * HD
    cost = pl.CostEstimate(
        flops=4 * n_q * (n_cache + n_new) * HD * heads,
        transcendentals=n_q * (n_cache + n_new) * heads,
        bytes_accessed=2 * (all_queries.size + cache_rows.size + new_rows.size) + 2 * n_q * width,
    )
    return pl.pallas_call(
        attend_kernel,
        out_shape=jax.ShapeDtypeStruct((n_q, width), jnp.bfloat16),
        grid_spec=pltpu.PrefetchScalarGridSpec(
            num_scalar_prefetch=1,
            grid=(KVH,),
            in_specs=[
                pl.BlockSpec((n_q, GROUP * HD), lambda k, s: (0, k)),
                pl.BlockSpec((n_cache, HD), lambda k, s: (0, k)),
                pl.BlockSpec((n_cache, HD), lambda k, s: (0, KVH + k)),
                pl.BlockSpec((n_new, HD), lambda k, s: (0, k)),
                pl.BlockSpec((n_new, HD), lambda k, s: (0, KVH + k)),
            ],
            out_specs=pl.BlockSpec((n_q, width), lambda k, s: (0, 0)),
        ),
        cost_estimate=cost,
    )(scal, all_queries, cache_rows, cache_rows, new_rows, new_rows)


def combine_kernel(got_ref, res_ref, w_ref, gain_ref, mixed_ref, normed_ref):
    heads = KVH * GROUP
    n_src = got_ref.shape[0]
    base = heads * HD
    stats = [got_ref[j, :, base : base + HD].astype(jnp.float32) for j in range(n_src)]
    tops = [st + pltpu.roll(st, HD - heads, 1) for st in stats]
    sums = [pltpu.roll(st, HD - 2 * heads, 1) + pltpu.roll(st, HD - 3 * heads, 1) for st in stats]
    top = tops[0]
    for t in tops[1:]:
        top = jnp.maximum(top, t)
    weights = [jnp.exp(t - top) for t in tops]
    total = weights[0] * sums[0]
    for w, s in zip(weights[1:], sums[1:]):
        total = total + w * s
    inverse = 1.0 / total
    inverse = inverse * (2.0 - total * inverse)
    scales = [w * inverse for w in weights]
    cols = []
    for h in range(heads):
        col = scales[0][:, h : h + 1] * got_ref[0, :, h * HD : (h + 1) * HD].astype(jnp.float32)
        for j in range(1, n_src):
            col = col + scales[j][:, h : h + 1] * got_ref[j, :, h * HD : (h + 1) * HD].astype(
                jnp.float32
            )
        cols.append(col.astype(jnp.bfloat16))
    attended = jnp.concatenate(cols, 1)
    mixed = (
        res_ref[...].astype(jnp.float32)
        + jnp.dot(attended, w_ref[...], preferred_element_type=jnp.float32)
    ).astype(jnp.bfloat16)
    mixed_ref[...] = mixed
    wide = mixed.astype(jnp.float32)
    square_mean = jnp.mean(wide * wide, -1, keepdims=True) + 1e-06
    root = lax.rsqrt(square_mean)
    root = root * (1.5 - 0.5 * square_mean * root * root)
    normed = wide * root * gain_ref[...]
    normed_ref[...] = normed.astype(jnp.bfloat16)


def combine_and_norm(got, residual, out_proj, norm_gain):
    rows, width = residual.shape
    out = jax.ShapeDtypeStruct((rows, width), jnp.bfloat16)
    cost = pl.CostEstimate(
        flops=2 * rows * out_proj.shape[0] * width,
        transcendentals=0,
        bytes_accessed=2 * (got.size + out_proj.size + 3 * residual.size),
    )
    return pl.pallas_call(
        combine_kernel,
        out_shape=(out, out),
        cost_estimate=cost,
    )(got, residual, out_proj, norm_gain.reshape(1, -1))


EXP_AXES = ("z", "x", "core")
CHIP_AXES = ("z", "x")


def local(
    residual_in,
    queries,
    new_kv,
    cache_kv,
    cache_len,
    out_proj,
    norm_gain,
    routes,
    route_w,
    w_gate_up,
    w_down,
):
    tok_count = residual_in.shape[1]
    cache_rows = cache_kv.shape[1]
    n_ctx = lax.axis_size("ctx")
    ctx_pos = lax.axis_index("ctx")
    length = cache_len[0]
    score_scale = HD ** (-0.5)
    heads = KVH * GROUP

    top_count = routes.shape[2]
    core_size = lax.axis_size("core")
    core_pos = lax.axis_index("core")
    expert_total = w_gate_up.shape[0] * lax.axis_size(EXP_AXES)
    capacity = min(tok_count, 3 * tok_count * top_count // (2 * expert_total))
    packed = jnp.concatenate(
        [
            routes[0].astype(jnp.bfloat16),
            route_w[0],
            jnp.zeros((tok_count, HD - 2 * top_count), jnp.bfloat16),
        ],
        -1,
    )
    both = lax.all_gather(packed, "core", axis=0, tiled=True)
    routes_both = both[:, :top_count].astype(jnp.int32)
    weights_both = both[:, top_count : 2 * top_count]
    expert_ids = routes_both.reshape(core_size, tok_count * top_count)
    pairs = expert_ids[:, :, None] == expert_ids[:, None, :]
    earlier = jnp.arange(tok_count * top_count)
    earlier = earlier[None, :] < earlier[:, None]
    slot_index = jnp.sum((pairs & earlier[None]).astype(jnp.int32), -1)
    block_rows = core_size * capacity
    source_core = jnp.arange(core_size)[:, None]
    dest = jnp.where(
        expert_ids % core_size == core_pos,
        ((expert_ids // core_size) * capacity + slot_index) * core_size + source_core,
        -1,
    ).reshape(core_size * tok_count, top_count)

    all_queries = lax.all_gather(queries[0], "ctx", axis=0, tiled=True)
    scal = jnp.stack([ctx_pos, length]).astype(jnp.int32)
    part = partial_attention(scal, all_queries, cache_kv[0], new_kv[0])
    got = lax.all_to_all(
        part.reshape(n_ctx, tok_count, part.shape[1]), "ctx", split_axis=0, concat_axis=0, tiled=True
    )
    mixed, normed = combine_and_norm(got, residual_in[0], out_proj, norm_gain)
    widened = mixed.astype(jnp.float32)

    normed_both = lax.all_gather(normed, "core", axis=0, tiled=True)
    chip_count = expert_total // core_size
    slot_ids = jnp.arange(chip_count * block_rows)
    hits = dest[None, :, :] == slot_ids[:, None, None]
    slot_shape = (chip_count, capacity, core_size)
    select = jnp.any(hits, -1).astype(jnp.bfloat16).reshape(*slot_shape, -1)
    outgoing = jnp.einsum(
        "jscr,rd->jscd", select, normed_both, preferred_element_type=jnp.float32
    ).astype(jnp.bfloat16)
    incoming = lax.all_to_all(outgoing, CHIP_AXES, split_axis=0, concat_axis=0, tiled=True)
    hidden_half = w_gate_up.shape[2] // 2
    gate_up = jnp.einsum("jscd,df->jscf", incoming, w_gate_up[0], preferred_element_type=jnp.float32)
    activated = (jax.nn.silu(gate_up[..., :hidden_half]) * gate_up[..., hidden_half:]).astype(
        jnp.bfloat16
    )
    result = jnp.einsum(
        "jscf,fd->jscd", activated, w_down[0], preferred_element_type=jnp.float32
    ).astype(jnp.bfloat16)
    returned = lax.all_to_all(result, CHIP_AXES, split_axis=0, concat_axis=0, tiled=True)
    combine = jnp.sum(
        jnp.where(
            hits.transpose(1, 0, 2), weights_both[:, None, :], jnp.zeros((), weights_both.dtype)
        ),
        -1,
    ).reshape(core_size, tok_count, *slot_shape)
    theirs = jnp.einsum(
        "tjsc,jscd->td", combine[1 - core_pos], returned, preferred_element_type=jnp.float32
    )
    sent = lax.ppermute(theirs, "core", [(0, 1), (1, 0)])
    mine = jnp.einsum(
        "tjsc,jscd->td", combine[core_pos], returned, preferred_element_type=jnp.float32
    )
    blended = lax.optimization_barrier(mine) + sent
    return (widened + blended).astype(jnp.bfloat16)[None]


def solution(mesh):
    exp_size = mesh.shape["exp"]
    x_size, core_size = 4, 2
    devices = mesh.devices.reshape(
        mesh.shape["ctx"], exp_size // (x_size * core_size), x_size, core_size
    )
    fine = Mesh(devices, ("ctx",) + EXP_AXES)
    rows = P(EXP_AXES, "ctx", None)
    return jax.shard_map(
        local,
        mesh=fine,
        in_specs=(
            rows,
            rows,
            rows,
            rows,
            P(EXP_AXES),
            P(),
            P(),
            rows,
            rows,
            P(EXP_AXES, None, None),
            P(EXP_AXES, None, None),
        ),
        out_specs=rows,
        check_vma=False,
    )
```

```python
import jax
import jax.numpy as jnp
from jax import lax
from jax.experimental import pallas as pl
from jax.experimental.pallas import tpu as pltpu
from jax.sharding import Mesh, PartitionSpec as P

D = 1536
KVH = 4
HD = 128
GROUP = 3


NEG_BIG = -1e30


def attend_kernel(scal_ref, q_ref, kc_ref, vc_ref, kn_ref, vn_ref, out_ref):
    kv_head = pl.program_id(0)
    heads = KVH * GROUP
    ctx_pos = scal_ref[0]
    length = scal_ref[1]
    scale = HD ** (-0.5)
    scale_log2 = scale * 1.4426950408889634
    n_q = q_ref.shape[0]
    q = jnp.concatenate([q_ref[:, g * HD : (g + 1) * HD] for g in range(GROUP)], 0)
    dims = (((1,), (1,)), ((), ()))
    s_c = lax.dot_general(q, kc_ref[...], dims, preferred_element_type=jnp.float32)
    s_n = lax.dot_general(q, kn_ref[...], dims, preferred_element_type=jnp.float32)
    n_rows, n_cache = s_c.shape
    n_new = s_n.shape[1]
    use_c = lax.broadcasted_iota(jnp.int32, (n_rows, n_cache), 1) < length - ctx_pos * n_cache
    causal = ctx_pos * n_new + lax.broadcasted_iota(jnp.int32, (n_q, n_new), 1) <= (
        lax.broadcasted_iota(jnp.int32, (n_q, n_new), 0)
    )
    use_n = jnp.concatenate([causal] * GROUP, 0)
    s_c = jnp.where(use_c, s_c, NEG_BIG)
    s_n = jnp.where(use_n, s_n, NEG_BIG)
    top = jnp.maximum(
        jnp.maximum(jnp.max(s_c, 1, keepdims=True), jnp.max(s_n, 1, keepdims=True)),
        NEG_BIG / 10,
    )
    p_c = jnp.exp2((s_c - top) * scale_log2)
    p_n = jnp.exp2((s_n - top) * scale_log2)
    top = top * scale
    total = jnp.sum(p_c, 1, keepdims=True) + jnp.sum(p_n, 1, keepdims=True)
    acc = jnp.dot(
        p_c.astype(jnp.bfloat16), vc_ref[...], preferred_element_type=jnp.float32
    ) + jnp.dot(p_n.astype(jnp.bfloat16), vn_ref[...], preferred_element_type=jnp.float32)
    stat_cols = slice(heads * HD, (heads + 1) * HD)

    @pl.when(kv_head == 0)
    def _():
        out_ref[:, stat_cols] = jnp.zeros((n_q, HD), out_ref.dtype)

    top_hi = top.astype(jnp.bfloat16).astype(jnp.float32)
    total_hi = total.astype(jnp.bfloat16).astype(jnp.float32)
    lane = lax.broadcasted_iota(jnp.int32, (n_q, HD), 1)
    held = out_ref[:, stat_cols].astype(jnp.float32)
    for g in range(GROUP):
        head = kv_head * GROUP + g
        rows = slice(g * n_q, (g + 1) * n_q)
        out_ref[:, pl.ds(pl.multiple_of(head * HD, HD), HD)] = acc[rows].astype(out_ref.dtype)
        held = jnp.where(lane == head, top_hi[rows], held)
        held = jnp.where(lane == heads + head, (top - top_hi)[rows], held)
        held = jnp.where(lane == 2 * heads + head, total_hi[rows], held)
        held = jnp.where(lane == 3 * heads + head, (total - total_hi)[rows], held)
    out_ref[:, stat_cols] = held.astype(out_ref.dtype)


def partial_attention(scal, all_queries, cache_rows, new_rows):
    n_q = all_queries.shape[0]
    n_cache = cache_rows.shape[0]
    n_new = new_rows.shape[0]
    heads = KVH * GROUP
    width = (heads + 1) * HD
    cost = pl.CostEstimate(
        flops=4 * n_q * (n_cache + n_new) * HD * heads,
        transcendentals=n_q * (n_cache + n_new) * heads,
        bytes_accessed=2 * (all_queries.size + cache_rows.size + new_rows.size) + 2 * n_q * width,
    )
    return pl.pallas_call(
        attend_kernel,
        out_shape=jax.ShapeDtypeStruct((n_q, width), jnp.bfloat16),
        grid_spec=pltpu.PrefetchScalarGridSpec(
            num_scalar_prefetch=1,
            grid=(KVH,),
            in_specs=[
                pl.BlockSpec((n_q, GROUP * HD), lambda k, s: (0, k)),
                pl.BlockSpec((n_cache, HD), lambda k, s: (0, k)),
                pl.BlockSpec((n_cache, HD), lambda k, s: (0, KVH + k)),
                pl.BlockSpec((n_new, HD), lambda k, s: (0, k)),
                pl.BlockSpec((n_new, HD), lambda k, s: (0, KVH + k)),
            ],
            out_specs=pl.BlockSpec((n_q, width), lambda k, s: (0, 0)),
        ),
        cost_estimate=cost,
    )(scal, all_queries, cache_rows, cache_rows, new_rows, new_rows)


def combine_kernel(got_ref, res_ref, w_ref, gain_ref, mixed_ref, normed_ref):
    heads = KVH * GROUP
    n_src = got_ref.shape[0]
    base = heads * HD
    stats = [got_ref[j, :, base : base + HD].astype(jnp.float32) for j in range(n_src)]
    tops = [st + pltpu.roll(st, HD - heads, 1) for st in stats]
    sums = [pltpu.roll(st, HD - 2 * heads, 1) + pltpu.roll(st, HD - 3 * heads, 1) for st in stats]
    top = tops[0]
    for t in tops[1:]:
        top = jnp.maximum(top, t)
    weights = [jnp.exp(t - top) for t in tops]
    total = weights[0] * sums[0]
    for w, s in zip(weights[1:], sums[1:]):
        total = total + w * s
    inverse = 1.0 / total
    inverse = inverse * (2.0 - total * inverse)
    scales = [w * inverse for w in weights]
    cols = []
    for h in range(heads):
        col = scales[0][:, h : h + 1] * got_ref[0, :, h * HD : (h + 1) * HD].astype(jnp.float32)
        for j in range(1, n_src):
            col = col + scales[j][:, h : h + 1] * got_ref[j, :, h * HD : (h + 1) * HD].astype(
                jnp.float32
            )
        cols.append(col.astype(jnp.bfloat16))
    attended = jnp.concatenate(cols, 1)
    mixed = (
        res_ref[...].astype(jnp.float32)
        + jnp.dot(attended, w_ref[...], preferred_element_type=jnp.float32)
    ).astype(jnp.bfloat16)
    mixed_ref[...] = mixed
    wide = mixed.astype(jnp.float32)
    square_mean = jnp.mean(wide * wide, -1, keepdims=True) + 1e-06
    root = lax.rsqrt(square_mean)
    root = root * (1.5 - 0.5 * square_mean * root * root)
    normed = wide * root * gain_ref[...]
    normed_ref[...] = normed.astype(jnp.bfloat16)


def combine_and_norm(got, residual, out_proj, norm_gain):
    rows, width = residual.shape
    out = jax.ShapeDtypeStruct((rows, width), jnp.bfloat16)
    cost = pl.CostEstimate(
        flops=2 * rows * out_proj.shape[0] * width,
        transcendentals=0,
        bytes_accessed=2 * (got.size + out_proj.size + 3 * residual.size),
    )
    return pl.pallas_call(
        combine_kernel,
        out_shape=(out, out),
        cost_estimate=cost,
    )(got, residual, out_proj, norm_gain.reshape(1, -1))


EXP_AXES = ("z", "x", "core")
CHIP_AXES = ("z", "x")


def local(
    residual_in,
    queries,
    new_kv,
    cache_kv,
    cache_len,
    out_proj,
    norm_gain,
    routes,
    route_w,
    w_gate_up,
    w_down,
):
    tok_count = residual_in.shape[1]
    cache_rows = cache_kv.shape[1]
    n_ctx = lax.axis_size("ctx")
    ctx_pos = lax.axis_index("ctx")
    length = cache_len[0]
    score_scale = HD ** (-0.5)
    heads = KVH * GROUP

    top_count = routes.shape[2]
    core_size = lax.axis_size("core")
    core_pos = lax.axis_index("core")
    expert_total = w_gate_up.shape[0] * lax.axis_size(EXP_AXES)
    capacity = min(tok_count, 3 * tok_count * top_count // (2 * expert_total))
    packed = jnp.concatenate(
        [
            routes[0].astype(jnp.bfloat16),
            route_w[0],
            jnp.zeros((tok_count, HD - 2 * top_count), jnp.bfloat16),
        ],
        -1,
    )
    both = lax.all_gather(packed, "core", axis=0, tiled=True)
    routes_both = both[:, :top_count].astype(jnp.int32)
    weights_both = both[:, top_count : 2 * top_count]
    expert_ids = routes_both.reshape(core_size, tok_count * top_count)
    pairs = expert_ids[:, :, None] == expert_ids[:, None, :]
    earlier = jnp.arange(tok_count * top_count)
    earlier = earlier[None, :] < earlier[:, None]
    slot_index = jnp.sum((pairs & earlier[None]).astype(jnp.int32), -1)
    block_rows = core_size * capacity
    source_core = jnp.arange(core_size)[:, None]
    dest = jnp.where(
        expert_ids % core_size == core_pos,
        ((expert_ids // core_size) * capacity + slot_index) * core_size + source_core,
        -1,
    ).reshape(core_size * tok_count, top_count)

    all_queries = lax.all_gather(queries[0], "ctx", axis=0, tiled=True)
    scal = jnp.stack([ctx_pos, length]).astype(jnp.int32)
    part = partial_attention(scal, all_queries, cache_kv[0], new_kv[0])
    got = lax.all_to_all(
        part.reshape(n_ctx, tok_count, part.shape[1]), "ctx", split_axis=0, concat_axis=0, tiled=True
    )
    mixed, normed = combine_and_norm(got, residual_in[0], out_proj, norm_gain)
    widened = mixed.astype(jnp.float32)

    partner_normed = lax.ppermute(normed, "core", [(0, 1), (1, 0)])
    chip_count = expert_total // core_size
    slot_ids = jnp.arange(chip_count * block_rows)
    hits = dest[None, :, :] == slot_ids[:, None, None]
    slot_shape = (chip_count, capacity, core_size)
    select = jnp.any(hits, -1).astype(jnp.bfloat16).reshape(*slot_shape, core_size, tok_count)
    own_rows = jnp.einsum(
        "jscr,rd->jscd", select[:, :, :, core_pos], normed, preferred_element_type=jnp.float32
    )
    partner_rows = jnp.einsum(
        "jscr,rd->jscd",
        select[:, :, :, 1 - core_pos],
        partner_normed,
        preferred_element_type=jnp.float32,
    )
    outgoing = (lax.optimization_barrier(own_rows) + partner_rows).astype(jnp.bfloat16)
    incoming = lax.all_to_all(outgoing, CHIP_AXES, split_axis=0, concat_axis=0, tiled=True)
    hidden_half = w_gate_up.shape[2] // 2
    gate_up = jnp.einsum("jscd,df->jscf", incoming, w_gate_up[0], preferred_element_type=jnp.float32)
    activated = (jax.nn.silu(gate_up[..., :hidden_half]) * gate_up[..., hidden_half:]).astype(
        jnp.bfloat16
    )
    result = jnp.einsum(
        "jscf,fd->jscd", activated, w_down[0], preferred_element_type=jnp.float32
    ).astype(jnp.bfloat16)
    returned = lax.all_to_all(result, CHIP_AXES, split_axis=0, concat_axis=0, tiled=True)
    combine = jnp.sum(
        jnp.where(
            hits.transpose(1, 0, 2), weights_both[:, None, :], jnp.zeros((), weights_both.dtype)
        ),
        -1,
    ).reshape(core_size, tok_count, *slot_shape)
    theirs = jnp.einsum(
        "tjsc,jscd->td", combine[1 - core_pos], returned, preferred_element_type=jnp.float32
    )
    sent = lax.ppermute(theirs, "core", [(0, 1), (1, 0)])
    mine = jnp.einsum(
        "tjsc,jscd->td", combine[core_pos], returned, preferred_element_type=jnp.float32
    )
    blended = lax.optimization_barrier(mine) + sent
    return (widened + blended).astype(jnp.bfloat16)[None]


def solution(mesh):
    exp_size = mesh.shape["exp"]
    x_size, core_size = 4, 2
    devices = mesh.devices.reshape(
        mesh.shape["ctx"], exp_size // (x_size * core_size), x_size, core_size
    )
    fine = Mesh(devices, ("ctx",) + EXP_AXES)
    rows = P(EXP_AXES, "ctx", None)
    return jax.shard_map(
        local,
        mesh=fine,
        in_specs=(
            rows,
            rows,
            rows,
            rows,
            P(EXP_AXES),
            P(),
            P(),
            rows,
            rows,
            P(EXP_AXES, None, None),
            P(EXP_AXES, None, None),
        ),
        out_specs=rows,
        check_vma=False,
    )
```

```python
import jax
import jax.numpy as jnp
from jax import lax
from jax.experimental import pallas as pl
from jax.experimental.pallas import tpu as pltpu
from jax.sharding import Mesh, PartitionSpec as P

D = 1536
KVH = 4
HD = 128
GROUP = 3


NEG_BIG = -1e30


def attend_kernel(scal_ref, q_ref, kc_ref, vc_ref, kn_ref, vn_ref, out_ref):
    kv_head = pl.program_id(0)
    heads = KVH * GROUP
    ctx_pos = scal_ref[0]
    length = scal_ref[1]
    scale = HD ** (-0.5)
    scale_log2 = scale * 1.4426950408889634
    n_q = q_ref.shape[0]
    q = jnp.concatenate([q_ref[:, g * HD : (g + 1) * HD] for g in range(GROUP)], 0)
    dims = (((1,), (1,)), ((), ()))
    s_c = lax.dot_general(q, kc_ref[...], dims, preferred_element_type=jnp.float32)
    s_n = lax.dot_general(q, kn_ref[...], dims, preferred_element_type=jnp.float32)
    n_rows, n_cache = s_c.shape
    n_new = s_n.shape[1]
    use_c = lax.broadcasted_iota(jnp.int32, (n_rows, n_cache), 1) < length - ctx_pos * n_cache
    causal = ctx_pos * n_new + lax.broadcasted_iota(jnp.int32, (n_q, n_new), 1) <= (
        lax.broadcasted_iota(jnp.int32, (n_q, n_new), 0)
    )
    use_n = jnp.concatenate([causal] * GROUP, 0)
    s_c = jnp.where(use_c, s_c, NEG_BIG)
    s_n = jnp.where(use_n, s_n, NEG_BIG)
    top = jnp.maximum(
        jnp.maximum(jnp.max(s_c, 1, keepdims=True), jnp.max(s_n, 1, keepdims=True)),
        NEG_BIG / 10,
    )
    p_c = jnp.exp2((s_c - top) * scale_log2)
    p_n = jnp.exp2((s_n - top) * scale_log2)
    top = top * scale
    total = jnp.sum(p_c, 1, keepdims=True) + jnp.sum(p_n, 1, keepdims=True)
    acc = jnp.dot(
        p_c.astype(jnp.bfloat16), vc_ref[...], preferred_element_type=jnp.float32
    ) + jnp.dot(p_n.astype(jnp.bfloat16), vn_ref[...], preferred_element_type=jnp.float32)
    stat_cols = slice(heads * HD, (heads + 1) * HD)

    @pl.when(kv_head == 0)
    def _():
        out_ref[:, stat_cols] = jnp.zeros((n_q, HD), out_ref.dtype)

    top_hi = top.astype(jnp.bfloat16).astype(jnp.float32)
    total_hi = total.astype(jnp.bfloat16).astype(jnp.float32)
    lane = lax.broadcasted_iota(jnp.int32, (n_q, HD), 1)
    held = out_ref[:, stat_cols].astype(jnp.float32)
    for g in range(GROUP):
        head = kv_head * GROUP + g
        rows = slice(g * n_q, (g + 1) * n_q)
        out_ref[:, pl.ds(pl.multiple_of(head * HD, HD), HD)] = acc[rows].astype(out_ref.dtype)
        held = jnp.where(lane == head, top_hi[rows], held)
        held = jnp.where(lane == heads + head, (top - top_hi)[rows], held)
        held = jnp.where(lane == 2 * heads + head, total_hi[rows], held)
        held = jnp.where(lane == 3 * heads + head, (total - total_hi)[rows], held)
    out_ref[:, stat_cols] = held.astype(out_ref.dtype)


def partial_attention(scal, all_queries, cache_rows, new_rows):
    n_q = all_queries.shape[0]
    n_cache = cache_rows.shape[0]
    n_new = new_rows.shape[0]
    heads = KVH * GROUP
    width = (heads + 1) * HD
    cost = pl.CostEstimate(
        flops=4 * n_q * (n_cache + n_new) * HD * heads,
        transcendentals=n_q * (n_cache + n_new) * heads,
        bytes_accessed=2 * (all_queries.size + cache_rows.size + new_rows.size) + 2 * n_q * width,
    )
    return pl.pallas_call(
        attend_kernel,
        out_shape=jax.ShapeDtypeStruct((n_q, width), jnp.bfloat16),
        grid_spec=pltpu.PrefetchScalarGridSpec(
            num_scalar_prefetch=1,
            grid=(KVH,),
            in_specs=[
                pl.BlockSpec((n_q, GROUP * HD), lambda k, s: (0, k)),
                pl.BlockSpec((n_cache, HD), lambda k, s: (0, k)),
                pl.BlockSpec((n_cache, HD), lambda k, s: (0, KVH + k)),
                pl.BlockSpec((n_new, HD), lambda k, s: (0, k)),
                pl.BlockSpec((n_new, HD), lambda k, s: (0, KVH + k)),
            ],
            out_specs=pl.BlockSpec((n_q, width), lambda k, s: (0, 0)),
        ),
        cost_estimate=cost,
    )(scal, all_queries, cache_rows, cache_rows, new_rows, new_rows)


def combine_kernel(got_ref, res_ref, w_hbm, gain_ref, mixed_ref, normed_ref, w_ref, w_sem):
    w_copy = pltpu.make_async_copy(w_hbm, w_ref, w_sem)
    w_copy.start()
    heads = KVH * GROUP
    n_src = got_ref.shape[0]
    base = heads * HD
    stats = [got_ref[j, :, base : base + HD].astype(jnp.float32) for j in range(n_src)]
    tops = [st + pltpu.roll(st, HD - heads, 1) for st in stats]
    sums = [pltpu.roll(st, HD - 2 * heads, 1) + pltpu.roll(st, HD - 3 * heads, 1) for st in stats]
    top = tops[0]
    for t in tops[1:]:
        top = jnp.maximum(top, t)
    weights = [jnp.exp(t - top) for t in tops]
    total = weights[0] * sums[0]
    for w, s in zip(weights[1:], sums[1:]):
        total = total + w * s
    inverse = 1.0 / total
    inverse = inverse * (2.0 - total * inverse)
    scales = [w * inverse for w in weights]
    cols = []
    for h in range(heads):
        col = scales[0][:, h : h + 1] * got_ref[0, :, h * HD : (h + 1) * HD].astype(jnp.float32)
        for j in range(1, n_src):
            col = col + scales[j][:, h : h + 1] * got_ref[j, :, h * HD : (h + 1) * HD].astype(
                jnp.float32
            )
        cols.append(col.astype(jnp.bfloat16))
    attended = jnp.concatenate(cols, 1)
    w_copy.wait()
    mixed = (
        res_ref[...].astype(jnp.float32)
        + jnp.dot(attended, w_ref[...], preferred_element_type=jnp.float32)
    ).astype(jnp.bfloat16)
    mixed_ref[...] = mixed
    wide = mixed.astype(jnp.float32)
    square_mean = jnp.mean(wide * wide, -1, keepdims=True) + 1e-06
    root = lax.rsqrt(square_mean)
    root = root * (1.5 - 0.5 * square_mean * root * root)
    normed = wide * root * gain_ref[...]
    normed_ref[...] = normed.astype(jnp.bfloat16)


def combine_and_norm(got, residual, out_proj, norm_gain):
    rows, width = residual.shape
    out = jax.ShapeDtypeStruct((rows, width), jnp.bfloat16)
    cost = pl.CostEstimate(
        flops=2 * rows * out_proj.shape[0] * width,
        transcendentals=0,
        bytes_accessed=2 * (got.size + out_proj.size + 3 * residual.size),
    )
    vmem = pl.BlockSpec(memory_space=pltpu.VMEM)
    return pl.pallas_call(
        combine_kernel,
        out_shape=(out, out),
        in_specs=[vmem, vmem, pl.BlockSpec(memory_space=pl.ANY), vmem],
        out_specs=(vmem, vmem),
        scratch_shapes=[
            pltpu.VMEM(out_proj.shape, out_proj.dtype),
            pltpu.SemaphoreType.DMA(()),
        ],
        cost_estimate=cost,
    )(got, residual, out_proj, norm_gain.reshape(1, -1))


EXP_AXES = ("z", "x", "core")
CHIP_AXES = ("z", "x")


def local(
    residual_in,
    queries,
    new_kv,
    cache_kv,
    cache_len,
    out_proj,
    norm_gain,
    routes,
    route_w,
    w_gate_up,
    w_down,
):
    tok_count = residual_in.shape[1]
    cache_rows = cache_kv.shape[1]
    n_ctx = lax.axis_size("ctx")
    ctx_pos = lax.axis_index("ctx")
    length = cache_len[0]
    score_scale = HD ** (-0.5)
    heads = KVH * GROUP

    top_count = routes.shape[2]
    core_size = lax.axis_size("core")
    core_pos = lax.axis_index("core")
    expert_total = w_gate_up.shape[0] * lax.axis_size(EXP_AXES)
    capacity = min(tok_count, 3 * tok_count * top_count // (2 * expert_total))
    packed = jnp.concatenate(
        [
            routes[0].astype(jnp.bfloat16),
            route_w[0],
            jnp.zeros((tok_count, HD - 2 * top_count), jnp.bfloat16),
        ],
        -1,
    )
    both = lax.all_gather(packed, "core", axis=0, tiled=True)
    routes_both = both[:, :top_count].astype(jnp.int32)
    weights_both = both[:, top_count : 2 * top_count]
    expert_ids = routes_both.reshape(core_size, tok_count * top_count)
    pairs = expert_ids[:, :, None] == expert_ids[:, None, :]
    earlier = jnp.arange(tok_count * top_count)
    earlier = earlier[None, :] < earlier[:, None]
    slot_index = jnp.sum((pairs & earlier[None]).astype(jnp.int32), -1)
    block_rows = core_size * capacity
    source_core = jnp.arange(core_size)[:, None]
    dest = jnp.where(
        expert_ids % core_size == core_pos,
        ((expert_ids // core_size) * capacity + slot_index) * core_size + source_core,
        -1,
    ).reshape(core_size * tok_count, top_count)

    all_queries = lax.all_gather(queries[0], "ctx", axis=0, tiled=True)
    scal = jnp.stack([ctx_pos, length]).astype(jnp.int32)
    part = partial_attention(scal, all_queries, cache_kv[0], new_kv[0])
    got = lax.all_to_all(
        part.reshape(n_ctx, tok_count, part.shape[1]), "ctx", split_axis=0, concat_axis=0, tiled=True
    )
    mixed, normed = combine_and_norm(got, residual_in[0], out_proj, norm_gain)
    widened = mixed.astype(jnp.float32)

    normed_both = lax.all_gather(normed, "core", axis=0, tiled=True)
    chip_count = expert_total // core_size
    slot_ids = jnp.arange(chip_count * block_rows)
    hits = dest[None, :, :] == slot_ids[:, None, None]
    slot_shape = (chip_count, capacity, core_size)
    select = jnp.any(hits, -1).astype(jnp.bfloat16).reshape(*slot_shape, -1)
    outgoing = jnp.einsum(
        "jscr,rd->jscd", select, normed_both, preferred_element_type=jnp.float32
    ).astype(jnp.bfloat16)
    incoming = lax.all_to_all(outgoing, CHIP_AXES, split_axis=0, concat_axis=0, tiled=True)
    hidden_half = w_gate_up.shape[2] // 2
    gate_up = jnp.einsum("jscd,df->jscf", incoming, w_gate_up[0], preferred_element_type=jnp.float32)
    activated = (jax.nn.silu(gate_up[..., :hidden_half]) * gate_up[..., hidden_half:]).astype(
        jnp.bfloat16
    )
    result = jnp.einsum(
        "jscf,fd->jscd", activated, w_down[0], preferred_element_type=jnp.float32
    ).astype(jnp.bfloat16)
    returned = lax.all_to_all(result, CHIP_AXES, split_axis=0, concat_axis=0, tiled=True)
    combine = jnp.sum(
        jnp.where(
            hits.transpose(1, 0, 2), weights_both[:, None, :], jnp.zeros((), weights_both.dtype)
        ),
        -1,
    ).reshape(core_size, tok_count, *slot_shape)
    theirs = jnp.einsum(
        "tjsc,jscd->td", combine[1 - core_pos], returned, preferred_element_type=jnp.float32
    )
    sent = lax.ppermute(theirs, "core", [(0, 1), (1, 0)])
    mine = jnp.einsum(
        "tjsc,jscd->td", combine[core_pos], returned, preferred_element_type=jnp.float32
    )
    blended = lax.optimization_barrier(mine) + sent
    return (widened + blended).astype(jnp.bfloat16)[None]


def solution(mesh):
    exp_size = mesh.shape["exp"]
    x_size, core_size = 4, 2
    devices = mesh.devices.reshape(
        mesh.shape["ctx"], exp_size // (x_size * core_size), x_size, core_size
    )
    fine = Mesh(devices, ("ctx",) + EXP_AXES)
    rows = P(EXP_AXES, "ctx", None)
    return jax.shard_map(
        local,
        mesh=fine,
        in_specs=(
            rows,
            rows,
            rows,
            rows,
            P(EXP_AXES),
            P(),
            P(),
            rows,
            rows,
            P(EXP_AXES, None, None),
            P(EXP_AXES, None, None),
        ),
        out_specs=rows,
        check_vma=False,
    )
```
